512 devices in a mesh: req: 64 (over z, x, core), tp: 8 (over y).
Axes of the slice: x: 4, y: 8, z: 8, core: 2. Of those that a mesh axis runs over, the one named last changes fastest.
Arguments:
- q_new: bfloat16 [4096, 5120], P('req', 'tp'), may hold values from -6 to 6
- k_new: bfloat16 [4096, 1024], P('req', 'tp'), may hold values from -15 to 15
- v_new: bfloat16 [4096, 1024], P('req', 'tp'), may hold values from -6 to 6
- k_cache: bfloat16 [1024, 128, 1024], P('req', None, 'tp'), may hold values from -16 to 16
- v_cache: bfloat16 [1024, 128, 1024], P('req', None, 'tp'), may hold values from -6 to 6
- lengths: int32 [32], replicated, may hold values from 1 to 4096, as said below
- page_table: int32 [32, 32], replicated, may hold values from -1 to 1023, as said below
- w_out: bfloat16 [5120, 5120], P('req', 'tp'), may hold values from -0.078125 to 0.078125
Outputs:
- attn_out: bfloat16 [4096, 5120], P('req')
The draws below stay inside these ranges and needn't reach their ends.
Inputs may be any that keep to these rules, and one draw needn't show every extreme that they name: `lengths`: the last request, 31, has exactly 4096 cached tokens; every request has at least one. `page_table`: request r uses ceil(lengths[r] / 128) logical pages. Its first ceil(ceil(lengths[r] / 128) / 2) logical pages lie among global pages 2r * 16 to (2r + 1) * 16 - 1, the rest among (2r + 1) * 16 to (2r + 2) * 16 - 1; distinct logical pages use distinct global pages; entries past a request's last page are -1.
All inputs are finite; a program needn't handle non-finite values.
Results may differ from the reference program's by a relative error of at most 0.024.
Values may be sent and summed in bfloat16 or wider, within the bound.
No kernel may reach another device: no remote copies, remote signals or barrier semaphores. Data moves between devices by JAX's collectives and lax.ppermute only.
A program may use at most 64 MiB of HBM per device.

```python
import math
import jax
import jax.numpy as jnp
from jax import lax

D = 5120
QH = 40
KVH = 8
HD = 128
GROUP = 5
NEW = 128
PAGE = 128
PAGES_DEV = 16
REQS = 32
TOKENS = 4096
LMAX = 4096
MAXP = 32
POOL = 1024
N_REQ = 64


def lengths_common(key):
    first_key = jax.random.fold_in(key, 7)
    drawn = jax.random.randint(first_key, (REQS,), 1, LMAX + 1)
    return jnp.where(jnp.arange(REQS) == REQS - 1, LMAX, drawn).astype(jnp.int32)


def draw_lengths(key, part):
    return lengths_common(key)


def draw_page_table(key, part):
    lengths = lengths_common(key)
    page_count = (lengths + PAGE - 1) // PAGE
    even_pages = (page_count + 1) // 2
    logical = jnp.arange(MAXP)
    row_keys = jax.random.split(jax.random.fold_in(key, 13), N_REQ)
    orders = jax.vmap(lambda one_key: jax.random.permutation(one_key, PAGES_DEV))(row_keys)
    on_odd = logical[None, :] >= even_pages[:, None]
    device_row = 2 * jnp.arange(REQS)[:, None] + on_odd.astype(jnp.int32)
    position = jnp.where(on_odd, logical[None, :] - even_pages[:, None], logical[None, :])
    position = jnp.clip(position, 0, PAGES_DEV - 1)
    slot = orders[device_row, position]
    global_page = device_row * PAGES_DEV + slot
    return jnp.where(logical[None, :] < page_count[:, None], global_page, -1).astype(jnp.int32)


def draw_q_new(key, part):
    base_key = jax.random.fold_in(key, 21)
    drawn = jnp.clip(jax.random.normal(base_key, (TOKENS, QH * HD), jnp.float32), -6.0, 6.0)
    return drawn.astype(jnp.bfloat16)


def draw_k_new(key, part):
    base_key = jax.random.fold_in(key, 23)
    drawn = jnp.clip(2.5 * jax.random.normal(base_key, (TOKENS, KVH * HD), jnp.float32), -15.0, 15.0)
    return drawn.astype(jnp.bfloat16)


def level_of(own_key, dims, pieces, smallest, high):
    def one(dim, shards_of):
        steps = jax.random.uniform(jax.random.fold_in(jax.random.fold_in(own_key, 6), dim), (shards_of,), jnp.float32, smallest / len(pieces), high / len(pieces))
        return jnp.repeat(jnp.exp(steps), dims[dim] // shards_of).reshape((-1,) + (1,) * (len(dims) - dim - 1))

    level = one(*pieces[0])
    for cut in pieces[1:]:
        level = level * one(*cut)
    return level


def bell_draw(stream_key, shape, width, reach, cuts=(), kind=jnp.bfloat16):
    factor_of = level_of(stream_key, shape, cuts, -0.22, 0.18) if cuts else 1.0
    entries = jax.random.normal(stream_key, shape, jnp.float32) * width * factor_of
    return jnp.minimum(jnp.maximum(entries, -reach), reach).astype(kind)


def setup_inputs(seed: int = 0) -> dict:
    streams_of = jax.random.split(jax.random.key(seed), 9)
    q_new = draw_q_new(jax.random.fold_in(streams_of[8], 71), 0)
    k_new = draw_k_new(jax.random.fold_in(streams_of[8], 71), 0)
    v_new = bell_draw(streams_of[2], (TOKENS, KVH * HD), 1.0, 6.0, ((0, 64), (1, 8)))
    k_cache = bell_draw(streams_of[3], (POOL, PAGE, KVH * HD), 2.5, 16.0, ((0, 64), (2, 8)))
    v_cache = bell_draw(streams_of[4], (POOL, PAGE, KVH * HD), 1.0, 6.0, ((0, 64), (2, 8)))
    lengths = draw_lengths(jax.random.fold_in(streams_of[8], 71), 0)
    page_table = draw_page_table(jax.random.fold_in(streams_of[8], 71), 0)
    w_out = bell_draw(streams_of[7], (D, QH * HD), (QH * HD) ** -0.5, 0.078125, ((0, 64), (1, 8)))
    return dict(q_new=q_new, k_new=k_new, v_new=v_new, k_cache=k_cache, v_cache=v_cache, lengths=lengths, page_table=page_table, w_out=w_out)


ROPE_BASE = 1000000.0

def rotate(values, places):
    inverse = 1.0 / ROPE_BASE ** (jnp.arange(0, HD, 2).astype(jnp.float32) / HD)
    angles = places.astype(jnp.float32)[:, None] * inverse[None, :]
    cosine = jnp.concatenate([jnp.cos(angles), jnp.cos(angles)], axis=-1)[:, None, :]
    sine = jnp.concatenate([jnp.sin(angles), jnp.sin(angles)], axis=-1)[:, None, :]
    first_half = values[..., :HD // 2]
    second_half = values[..., HD // 2:]
    turned = jnp.concatenate([-second_half, first_half], axis=-1)
    return values * cosine + turned * sine

def reference(q_new, k_new, v_new, k_cache, v_cache, lengths, page_table, w_out):
    scale = 1.0 / math.sqrt(HD)
    queries = q_new.reshape(REQS, NEW, QH, HD)
    fresh_keys = k_new.reshape(REQS, NEW, KVH, HD)
    fresh_values = v_new.reshape(REQS, NEW, KVH, HD)
    pool_keys = k_cache.reshape(POOL, PAGE, KVH, HD)
    pool_values = v_cache.reshape(POOL, PAGE, KVH, HD)

    def one_request(items):
        query, key_new, value_new, length, table_row = items
        places = length + jnp.arange(NEW).astype(jnp.int32)
        query_rot = rotate(query.astype(jnp.float32), places).astype(jnp.bfloat16)
        query_rot = query_rot.reshape(NEW, KVH, GROUP, HD)
        key_rot = rotate(key_new.astype(jnp.float32), places).astype(jnp.bfloat16)
        slots = jnp.clip(table_row, 0, POOL - 1)
        cached_keys = pool_keys[slots].reshape(MAXP * PAGE, KVH, HD)
        cached_values = pool_values[slots].reshape(MAXP * PAGE, KVH, HD)
        all_keys = jnp.concatenate([cached_keys, key_rot], axis=0)
        all_values = jnp.concatenate([cached_values, value_new], axis=0)
        cache_index = jnp.arange(MAXP * PAGE).astype(jnp.int32)
        key_places = jnp.concatenate([cache_index, places])
        usable = jnp.concatenate([cache_index < length, jnp.ones((NEW,), bool)])
        allowed = usable[None, :] & (key_places[None, :] <= places[:, None])

        def one_head(head_items):
            head_query, head_keys, head_values = head_items
            scores = jnp.einsum('qgd,kd->gqk', head_query.astype(jnp.float32), head_keys.astype(jnp.float32)) * scale
            scores = jnp.where(allowed[None], scores, -jnp.inf)
            highest = lax.optimization_barrier(jnp.max(scores, axis=-1, keepdims=True))
            weights = jnp.exp(scores - highest)
            total = lax.optimization_barrier(jnp.sum(weights, axis=-1))
            rounded = lax.optimization_barrier(weights.astype(jnp.bfloat16))
            mixed = jnp.einsum('gqk,kd->qgd', rounded.astype(jnp.float32), head_values.astype(jnp.float32))
            return mixed / jnp.transpose(total)[..., None]
        heads = lax.map(one_head, (jnp.moveaxis(query_rot, 1, 0), jnp.moveaxis(all_keys, 1, 0), jnp.moveaxis(all_values, 1, 0)))
        return jnp.moveaxis(heads, 0, 1).reshape(NEW, QH * HD).astype(jnp.bfloat16)
    attention = lax.map(one_request, (queries, fresh_keys, fresh_values, lengths, page_table))
    attention = attention.reshape(TOKENS, QH * HD)
    return jnp.dot(attention, w_out.T, preferred_element_type=jnp.float32).astype(jnp.bfloat16)
```

```python
import math

import jax
import jax.numpy as jnp
from jax import lax
from jax.sharding import PartitionSpec as P

HD = 128
GROUP = 5
BLOCK_PAGES = 4


ROPE_BASE = 1000000.0
FLOOR_SCORE = -1e30


def from_partner(value, axis, distance):
    return lax.ppermute(value, axis, [(i, i ^ 1 << distance) for i in range(lax.axis_size(axis))])


def rotate(values, places):
    inverse = 1.0 / ROPE_BASE ** (jnp.arange(0, HD, 2).astype(jnp.float32) / HD)
    angles = places.astype(jnp.float32)[:, None] * inverse[None, :]
    cosine = jnp.concatenate([jnp.cos(angles), jnp.cos(angles)], axis=-1)[:, None, :]
    sine = jnp.concatenate([jnp.sin(angles), jnp.sin(angles)], axis=-1)[:, None, :]
    first_half = values[..., : HD // 2]
    second_half = values[..., HD // 2 :]
    turned = jnp.concatenate([-second_half, first_half], axis=-1)
    return values * cosine + turned * sine


def absorb(state, queries, block_keys, block_values, allowed, scale):
    running_max, running_sum, output = state
    scores = (
        jnp.einsum("qcgd,kcd->cgqk", queries, block_keys, preferred_element_type=jnp.float32)
        * scale
    )
    scores = jnp.where(allowed[None, None], scores, FLOOR_SCORE)
    new_max = jnp.maximum(running_max, jnp.max(scores, axis=-1))
    factor = jnp.exp(running_max - new_max)
    weights = jnp.where(allowed[None, None], jnp.exp(scores - new_max[..., None]), 0.0)
    running_sum = running_sum * factor + jnp.sum(weights, axis=-1)
    mixed = jnp.einsum(
        "cgqk,kcd->qcgd",
        weights.astype(jnp.bfloat16),
        block_values,
        preferred_element_type=jnp.float32,
    )
    output = output * jnp.transpose(factor, (2, 0, 1))[..., None] + mixed
    return (new_max, running_sum, output)


def tensor_total(partial_value):
    return lax.psum(partial_value.astype(jnp.bfloat16), "tp")


def shards(q_new, k_new, v_new, k_cache, v_cache, lengths, page_table, w_out):
    own_rows = q_new.shape[0]
    all_rows = 2 * own_rows
    local_heads = k_new.shape[1] // HD
    pages_local = k_cache.shape[0]
    page_rows = k_cache.shape[1]
    block_rows = BLOCK_PAGES * page_rows
    scale = 1.0 / math.sqrt(HD)
    weights_all = lax.all_gather(w_out, "req", axis=0, tiled=True)
    device_row = lax.axis_index("req")
    parity = device_row % 2
    request = device_row // 2
    length = lengths[request]
    own_places = length + parity * own_rows + jnp.arange(own_rows)
    own_queries = rotate(
        q_new.reshape(own_rows, local_heads * GROUP, HD).astype(jnp.float32), own_places
    ).astype(jnp.bfloat16)
    own_keys = rotate(
        k_new.reshape(own_rows, local_heads, HD).astype(jnp.float32), own_places
    ).astype(jnp.bfloat16)
    own_values = v_new.reshape(own_rows, local_heads, HD)
    peer_queries, peer_keys, peer_values = from_partner(
        (own_queries, own_keys, own_values), "req", 0
    )

    def ordered(mine, theirs):
        return jnp.where(
            parity == 0,
            jnp.concatenate([mine, theirs], axis=0),
            jnp.concatenate([theirs, mine], axis=0),
        )

    queries = ordered(own_queries, peer_queries).reshape(all_rows, local_heads, GROUP, HD)
    fresh_keys = ordered(own_keys, peer_keys)
    fresh_values = ordered(own_values, peer_values)
    state = (
        jnp.full((local_heads, GROUP, all_rows), FLOOR_SCORE, jnp.float32),
        jnp.zeros((local_heads, GROUP, all_rows), jnp.float32),
        jnp.zeros((all_rows, local_heads, GROUP, HD), jnp.float32),
    )
    token_index = jnp.arange(all_rows)
    causal = (token_index[None, :] <= token_index[:, None]) & (parity == 1)
    state = absorb(state, queries, fresh_keys, fresh_values, causal, scale)
    page_count = (length + page_rows - 1) // page_rows
    even_pages = (page_count + 1) // 2
    first_page = jnp.where(parity == 0, 0, even_pages)
    last_page = jnp.where(parity == 0, even_pages, page_count)
    table_row = jnp.concatenate([page_table[request], jnp.full((BLOCK_PAGES,), -1, jnp.int32)])
    offset = device_row * pages_local
    block_count = (last_page - first_page + BLOCK_PAGES - 1) // BLOCK_PAGES

    def visit(block, carry):
        block_first = first_page + block * BLOCK_PAGES
        logical = block_first + jnp.arange(BLOCK_PAGES)
        physical = lax.dynamic_slice(table_row, (block_first,), (BLOCK_PAGES,))
        slots = jnp.clip(physical - offset, 0, pages_local - 1)
        block_keys = k_cache[slots].reshape(block_rows, local_heads, HD)
        block_values = v_cache[slots].reshape(block_rows, local_heads, HD)
        key_places = (logical[:, None] * page_rows + jnp.arange(page_rows)[None, :]).reshape(
            block_rows
        )
        usable = jnp.repeat(logical < last_page, page_rows) & (key_places < length)
        allowed = jnp.broadcast_to(usable[None, :], (all_rows, block_rows))
        return absorb(carry, queries, block_keys, block_values, allowed, scale)

    running_max, running_sum, output = lax.fori_loop(0, block_count, visit, state)
    peer_start = (1 - parity) * own_rows
    own_start = parity * own_rows
    outgoing = (
        lax.dynamic_slice_in_dim(output, peer_start, own_rows, 0),
        lax.dynamic_slice_in_dim(running_max, peer_start, own_rows, 2),
        lax.dynamic_slice_in_dim(running_sum, peer_start, own_rows, 2),
    )
    other_output, other_max, other_sum = (
        from_partner(outgoing[0].astype(jnp.bfloat16), "req", 0).astype(jnp.float32),
        from_partner(outgoing[1].astype(jnp.bfloat16), "req", 0).astype(jnp.float32),
        from_partner(outgoing[2].astype(jnp.bfloat16), "req", 0).astype(jnp.float32),
    )
    mine_output = lax.dynamic_slice_in_dim(output, own_start, own_rows, 0)
    mine_max = lax.dynamic_slice_in_dim(running_max, own_start, own_rows, 2)
    mine_sum = lax.dynamic_slice_in_dim(running_sum, own_start, own_rows, 2)
    joint_max = jnp.maximum(mine_max, other_max)
    mine_factor = jnp.exp(mine_max - joint_max)
    other_factor = jnp.exp(other_max - joint_max)
    joint_sum = mine_sum * mine_factor + other_sum * other_factor
    joint_output = (
        mine_output * jnp.transpose(mine_factor, (2, 0, 1))[..., None]
        + other_output * jnp.transpose(other_factor, (2, 0, 1))[..., None]
    )
    attention = (
        (joint_output / jnp.transpose(joint_sum, (2, 0, 1))[..., None])
        .reshape(own_rows, local_heads * GROUP * HD)
        .astype(jnp.bfloat16)
    )
    partial_value = lax.dot_general(
        attention,
        weights_all,
        (((1,), (1,)), ((), ())),
        preferred_element_type=jnp.float32,
    )
    return tensor_total(partial_value)


def solution(mesh):
    in_specs = (
        P("req", "tp"),
        P("req", "tp"),
        P("req", "tp"),
        P("req", None, "tp"),
        P("req", None, "tp"),
        P(),
        P(),
        P("req", "tp"),
    )
    out_specs = P("req", None)
    return jax.shard_map(shards, mesh=mesh, in_specs=in_specs, out_specs=out_specs, check_vma=False)
```

```python
import math

import jax
import jax.numpy as jnp
from jax import lax
from jax.sharding import PartitionSpec as P

HD = 128
GROUP = 5
BLOCK_PAGES = 4


ROPE_BASE = 1000000.0
FLOOR_SCORE = -1e30


def from_partner(value, axis, distance):
    return lax.ppermute(value, axis, [(i, i ^ 1 << distance) for i in range(lax.axis_size(axis))])


def rotate(values, places):
    inverse = 1.0 / ROPE_BASE ** (jnp.arange(0, HD, 2).astype(jnp.float32) / HD)
    angles = places.astype(jnp.float32)[:, None] * inverse[None, :]
    cosine = jnp.concatenate([jnp.cos(angles), jnp.cos(angles)], axis=-1)[:, None, :]
    sine = jnp.concatenate([jnp.sin(angles), jnp.sin(angles)], axis=-1)[:, None, :]
    first_half = values[..., : HD // 2]
    second_half = values[..., HD // 2 :]
    turned = jnp.concatenate([-second_half, first_half], axis=-1)
    return values * cosine + turned * sine


def absorb(state, queries, block_keys, block_values, allowed, scale):
    running_max, running_sum, output = state
    scores = (
        jnp.einsum("qcgd,kcd->cgqk", queries, block_keys, preferred_element_type=jnp.float32)
        * scale
    )
    scores = jnp.where(allowed[None, None], scores, FLOOR_SCORE)
    new_max = jnp.maximum(running_max, jnp.max(scores, axis=-1))
    factor = jnp.exp(running_max - new_max)
    weights = jnp.where(allowed[None, None], jnp.exp(scores - new_max[..., None]), 0.0)
    running_sum = running_sum * factor + jnp.sum(weights, axis=-1)
    mixed = jnp.einsum(
        "cgqk,kcd->qcgd",
        weights.astype(jnp.bfloat16),
        block_values,
        preferred_element_type=jnp.float32,
    )
    output = output * jnp.transpose(factor, (2, 0, 1))[..., None] + mixed
    return (new_max, running_sum, output)


def tensor_total(partial_value):
    rows, features = partial_value.shape
    parts = lax.axis_size("tp")
    pieces = partial_value.astype(jnp.bfloat16).reshape(rows, parts, features // parts)
    pieces = lax.all_to_all(pieces, "tp", 1, 1, tiled=True)
    summed = jnp.sum(pieces.astype(jnp.float32), axis=1).astype(jnp.bfloat16)
    return lax.all_gather(summed, "tp", axis=1, tiled=True)


def shards(q_new, k_new, v_new, k_cache, v_cache, lengths, page_table, w_out):
    own_rows = q_new.shape[0]
    all_rows = 2 * own_rows
    local_heads = k_new.shape[1] // HD
    pages_local = k_cache.shape[0]
    page_rows = k_cache.shape[1]
    block_rows = BLOCK_PAGES * page_rows
    scale = 1.0 / math.sqrt(HD)
    weights_all = lax.all_gather(w_out, "req", axis=0, tiled=True)
    device_row = lax.axis_index("req")
    parity = device_row % 2
    request = device_row // 2
    length = lengths[request]
    own_places = length + parity * own_rows + jnp.arange(own_rows)
    own_queries = rotate(
        q_new.reshape(own_rows, local_heads * GROUP, HD).astype(jnp.float32), own_places
    ).astype(jnp.bfloat16)
    own_keys = rotate(
        k_new.reshape(own_rows, local_heads, HD).astype(jnp.float32), own_places
    ).astype(jnp.bfloat16)
    own_values = v_new.reshape(own_rows, local_heads, HD)
    peer_queries, peer_keys, peer_values = from_partner(
        (own_queries, own_keys, own_values), "req", 0
    )

    def ordered(mine, theirs):
        return jnp.where(
            parity == 0,
            jnp.concatenate([mine, theirs], axis=0),
            jnp.concatenate([theirs, mine], axis=0),
        )

    queries = ordered(own_queries, peer_queries).reshape(all_rows, local_heads, GROUP, HD)
    fresh_keys = ordered(own_keys, peer_keys)
    fresh_values = ordered(own_values, peer_values)
    state = (
        jnp.full((local_heads, GROUP, all_rows), FLOOR_SCORE, jnp.float32),
        jnp.zeros((local_heads, GROUP, all_rows), jnp.float32),
        jnp.zeros((all_rows, local_heads, GROUP, HD), jnp.float32),
    )
    token_index = jnp.arange(all_rows)
    causal = (token_index[None, :] <= token_index[:, None]) & (parity == 1)
    state = absorb(state, queries, fresh_keys, fresh_values, causal, scale)
    page_count = (length + page_rows - 1) // page_rows
    even_pages = (page_count + 1) // 2
    first_page = jnp.where(parity == 0, 0, even_pages)
    last_page = jnp.where(parity == 0, even_pages, page_count)
    table_row = jnp.concatenate([page_table[request], jnp.full((BLOCK_PAGES,), -1, jnp.int32)])
    offset = device_row * pages_local
    block_count = (last_page - first_page + BLOCK_PAGES - 1) // BLOCK_PAGES

    def visit(block, carry):
        block_first = first_page + block * BLOCK_PAGES
        logical = block_first + jnp.arange(BLOCK_PAGES)
        physical = lax.dynamic_slice(table_row, (block_first,), (BLOCK_PAGES,))
        slots = jnp.clip(physical - offset, 0, pages_local - 1)
        block_keys = k_cache[slots].reshape(block_rows, local_heads, HD)
        block_values = v_cache[slots].reshape(block_rows, local_heads, HD)
        key_places = (logical[:, None] * page_rows + jnp.arange(page_rows)[None, :]).reshape(
            block_rows
        )
        usable = jnp.repeat(logical < last_page, page_rows) & (key_places < length)
        allowed = jnp.broadcast_to(usable[None, :], (all_rows, block_rows))
        return absorb(carry, queries, block_keys, block_values, allowed, scale)

    running_max, running_sum, output = lax.fori_loop(0, block_count, visit, state)
    peer_start = (1 - parity) * own_rows
    own_start = parity * own_rows
    outgoing = (
        lax.dynamic_slice_in_dim(output, peer_start, own_rows, 0),
        lax.dynamic_slice_in_dim(running_max, peer_start, own_rows, 2),
        lax.dynamic_slice_in_dim(running_sum, peer_start, own_rows, 2),
    )
    other_output, other_max, other_sum = (
        from_partner(outgoing[0].astype(jnp.bfloat16), "req", 0).astype(jnp.float32),
        from_partner(outgoing[1].astype(jnp.bfloat16), "req", 0).astype(jnp.float32),
        from_partner(outgoing[2].astype(jnp.bfloat16), "req", 0).astype(jnp.float32),
    )
    mine_output = lax.dynamic_slice_in_dim(output, own_start, own_rows, 0)
    mine_max = lax.dynamic_slice_in_dim(running_max, own_start, own_rows, 2)
    mine_sum = lax.dynamic_slice_in_dim(running_sum, own_start, own_rows, 2)
    joint_max = jnp.maximum(mine_max, other_max)
    mine_factor = jnp.exp(mine_max - joint_max)
    other_factor = jnp.exp(other_max - joint_max)
    joint_sum = mine_sum * mine_factor + other_sum * other_factor
    joint_output = (
        mine_output * jnp.transpose(mine_factor, (2, 0, 1))[..., None]
        + other_output * jnp.transpose(other_factor, (2, 0, 1))[..., None]
    )
    attention = (
        (joint_output / jnp.transpose(joint_sum, (2, 0, 1))[..., None])
        .reshape(own_rows, local_heads * GROUP * HD)
        .astype(jnp.bfloat16)
    )
    partial_value = lax.dot_general(
        attention,
        weights_all,
        (((1,), (1,)), ((), ())),
        preferred_element_type=jnp.float32,
    )
    return tensor_total(partial_value)


def solution(mesh):
    in_specs = (
        P("req", "tp"),
        P("req", "tp"),
        P("req", "tp"),
        P("req", None, "tp"),
        P("req", None, "tp"),
        P(),
        P(),
        P("req", "tp"),
    )
    out_specs = P("req", None)
    return jax.shard_map(shards, mesh=mesh, in_specs=in_specs, out_specs=out_specs, check_vma=False)
```

```python
import math

import jax
import jax.numpy as jnp
from jax import lax
from jax.sharding import PartitionSpec as P

HD = 128
GROUP = 5
BLOCK_PAGES = 4


ROPE_BASE = 1000000.0
FLOOR_SCORE = -1e30


def from_partner(value, axis, distance):
    return lax.ppermute(value, axis, [(i, i ^ 1 << distance) for i in range(lax.axis_size(axis))])


def rotate(values, places):
    inverse = 1.0 / ROPE_BASE ** (jnp.arange(0, HD, 2).astype(jnp.float32) / HD)
    angles = places.astype(jnp.float32)[:, None] * inverse[None, :]
    cosine = jnp.concatenate([jnp.cos(angles), jnp.cos(angles)], axis=-1)[:, None, :]
    sine = jnp.concatenate([jnp.sin(angles), jnp.sin(angles)], axis=-1)[:, None, :]
    first_half = values[..., : HD // 2]
    second_half = values[..., HD // 2 :]
    turned = jnp.concatenate([-second_half, first_half], axis=-1)
    return values * cosine + turned * sine


def absorb(state, queries, block_keys, block_values, allowed, scale):
    running_max, running_sum, output = state
    scores = (
        jnp.einsum("qcgd,kcd->cgqk", queries, block_keys, preferred_element_type=jnp.float32)
        * scale
    )
    scores = jnp.where(allowed[None, None], scores, FLOOR_SCORE)
    new_max = jnp.maximum(running_max, jnp.max(scores, axis=-1))
    factor = jnp.exp(running_max - new_max)
    weights = jnp.where(allowed[None, None], jnp.exp(scores - new_max[..., None]), 0.0)
    running_sum = running_sum * factor + jnp.sum(weights, axis=-1)
    mixed = jnp.einsum(
        "cgqk,kcd->qcgd",
        weights.astype(jnp.bfloat16),
        block_values,
        preferred_element_type=jnp.float32,
    )
    output = output * jnp.transpose(factor, (2, 0, 1))[..., None] + mixed
    return (new_max, running_sum, output)


def output_rows(w_out):
    parts = lax.axis_size("tp")
    rows, width = w_out.shape
    share = rows // parts
    pieces = lax.all_to_all(w_out.reshape(parts, share, width), "tp", 0, 0, tiled=True)
    mine = jnp.transpose(pieces, (1, 0, 2)).reshape(share, parts * width)
    return lax.all_gather(mine, "req", axis=0)


def shards(q_new, k_new, v_new, k_cache, v_cache, lengths, page_table, w_out):
    own_rows = q_new.shape[0]
    all_rows = 2 * own_rows
    local_heads = k_new.shape[1] // HD
    pages_local = k_cache.shape[0]
    page_rows = k_cache.shape[1]
    block_rows = BLOCK_PAGES * page_rows
    scale = 1.0 / math.sqrt(HD)
    weights_mine = output_rows(w_out)
    device_row = lax.axis_index("req")
    parity = device_row % 2
    request = device_row // 2
    length = lengths[request]
    own_places = length + parity * own_rows + jnp.arange(own_rows)
    own_queries = rotate(
        q_new.reshape(own_rows, local_heads * GROUP, HD).astype(jnp.float32), own_places
    ).astype(jnp.bfloat16)
    own_keys = rotate(
        k_new.reshape(own_rows, local_heads, HD).astype(jnp.float32), own_places
    ).astype(jnp.bfloat16)
    own_values = v_new.reshape(own_rows, local_heads, HD)
    peer_queries, peer_keys, peer_values = from_partner(
        (own_queries, own_keys, own_values), "req", 0
    )

    def ordered(mine, theirs):
        return jnp.where(
            parity == 0,
            jnp.concatenate([mine, theirs], axis=0),
            jnp.concatenate([theirs, mine], axis=0),
        )

    queries = ordered(own_queries, peer_queries).reshape(all_rows, local_heads, GROUP, HD)
    fresh_keys = ordered(own_keys, peer_keys)
    fresh_values = ordered(own_values, peer_values)
    state = (
        jnp.full((local_heads, GROUP, all_rows), FLOOR_SCORE, jnp.float32),
        jnp.zeros((local_heads, GROUP, all_rows), jnp.float32),
        jnp.zeros((all_rows, local_heads, GROUP, HD), jnp.float32),
    )
    token_index = jnp.arange(all_rows)
    causal = (token_index[None, :] <= token_index[:, None]) & (parity == 1)
    state = absorb(state, queries, fresh_keys, fresh_values, causal, scale)
    page_count = (length + page_rows - 1) // page_rows
    even_pages = (page_count + 1) // 2
    first_page = jnp.where(parity == 0, 0, even_pages)
    last_page = jnp.where(parity == 0, even_pages, page_count)
    table_row = jnp.concatenate([page_table[request], jnp.full((BLOCK_PAGES,), -1, jnp.int32)])
    offset = device_row * pages_local
    block_count = (last_page - first_page + BLOCK_PAGES - 1) // BLOCK_PAGES

    def visit(block, carry):
        block_first = first_page + block * BLOCK_PAGES
        logical = block_first + jnp.arange(BLOCK_PAGES)
        physical = lax.dynamic_slice(table_row, (block_first,), (BLOCK_PAGES,))
        slots = jnp.clip(physical - offset, 0, pages_local - 1)
        block_keys = k_cache[slots].reshape(block_rows, local_heads, HD)
        block_values = v_cache[slots].reshape(block_rows, local_heads, HD)
        key_places = (logical[:, None] * page_rows + jnp.arange(page_rows)[None, :]).reshape(
            block_rows
        )
        usable = jnp.repeat(logical < last_page, page_rows) & (key_places < length)
        allowed = jnp.broadcast_to(usable[None, :], (all_rows, block_rows))
        return absorb(carry, queries, block_keys, block_values, allowed, scale)

    running_max, running_sum, output = lax.fori_loop(0, block_count, visit, state)
    peer_start = (1 - parity) * own_rows
    own_start = parity * own_rows
    outgoing = (
        lax.dynamic_slice_in_dim(output, peer_start, own_rows, 0),
        lax.dynamic_slice_in_dim(running_max, peer_start, own_rows, 2),
        lax.dynamic_slice_in_dim(running_sum, peer_start, own_rows, 2),
    )
    other_output, other_max, other_sum = (
        from_partner(outgoing[0].astype(jnp.bfloat16), "req", 0).astype(jnp.float32),
        from_partner(outgoing[1].astype(jnp.bfloat16), "req", 0).astype(jnp.float32),
        from_partner(outgoing[2].astype(jnp.bfloat16), "req", 0).astype(jnp.float32),
    )
    mine_output = lax.dynamic_slice_in_dim(output, own_start, own_rows, 0)
    mine_max = lax.dynamic_slice_in_dim(running_max, own_start, own_rows, 2)
    mine_sum = lax.dynamic_slice_in_dim(running_sum, own_start, own_rows, 2)
    joint_max = jnp.maximum(mine_max, other_max)
    mine_factor = jnp.exp(mine_max - joint_max)
    other_factor = jnp.exp(other_max - joint_max)
    joint_sum = mine_sum * mine_factor + other_sum * other_factor
    joint_output = (
        mine_output * jnp.transpose(mine_factor, (2, 0, 1))[..., None]
        + other_output * jnp.transpose(other_factor, (2, 0, 1))[..., None]
    )
    attention = (
        (joint_output / jnp.transpose(joint_sum, (2, 0, 1))[..., None])
        .reshape(own_rows, local_heads * GROUP * HD)
        .astype(jnp.bfloat16)
    )
    full_rows = lax.all_gather(attention, "tp", axis=1, tiled=True)
    projected = jnp.einsum(
        "qc,irc->qir", full_rows, weights_mine, preferred_element_type=jnp.float32
    ).astype(jnp.bfloat16)
    gathered = lax.all_gather(projected, "tp", axis=2, tiled=True)
    return gathered.reshape(own_rows, -1)


def solution(mesh):
    in_specs = (
        P("req", "tp"),
        P("req", "tp"),
        P("req", "tp"),
        P("req", None, "tp"),
        P("req", None, "tp"),
        P(),
        P(),
        P("req", "tp"),
    )
    out_specs = P("req", None)
    return jax.shard_map(shards, mesh=mesh, in_specs=in_specs, out_specs=out_specs, check_vma=False)
```

```python
import math

import jax
import jax.numpy as jnp
from jax import lax
from jax.sharding import PartitionSpec as P

HD = 128
GROUP = 5
BLOCK_PAGES = 4


ROPE_BASE = 1000000.0
FLOOR_SCORE = -1e30


def from_partner(value, axis, distance):
    return lax.ppermute(value, axis, [(i, i ^ 1 << distance) for i in range(lax.axis_size(axis))])


def rotate(values, places):
    inverse = 1.0 / ROPE_BASE ** (jnp.arange(0, HD, 2).astype(jnp.float32) / HD)
    angles = places.astype(jnp.float32)[:, None] * inverse[None, :]
    cosine = jnp.concatenate([jnp.cos(angles), jnp.cos(angles)], axis=-1)[:, None, :]
    sine = jnp.concatenate([jnp.sin(angles), jnp.sin(angles)], axis=-1)[:, None, :]
    first_half = values[..., : HD // 2]
    second_half = values[..., HD // 2 :]
    turned = jnp.concatenate([-second_half, first_half], axis=-1)
    return values * cosine + turned * sine


def absorb(state, queries, block_keys, block_values, allowed, scale):
    running_max, running_sum, output = state
    scores = (
        jnp.einsum("qcgd,kcd->cgqk", queries, block_keys, preferred_element_type=jnp.float32)
        * scale
    )
    scores = jnp.where(allowed[None, None], scores, FLOOR_SCORE)
    new_max = jnp.maximum(running_max, jnp.max(scores, axis=-1))
    factor = jnp.exp(running_max - new_max)
    weights = jnp.where(allowed[None, None], jnp.exp(scores - new_max[..., None]), 0.0)
    running_sum = running_sum * factor + jnp.sum(weights, axis=-1)
    mixed = jnp.einsum(
        "cgqk,kcd->qcgd",
        weights.astype(jnp.bfloat16),
        block_values,
        preferred_element_type=jnp.float32,
    )
    output = output * jnp.transpose(factor, (2, 0, 1))[..., None] + mixed
    return (new_max, running_sum, output)


def output_rows(w_out):
    parts = lax.axis_size("tp")
    rows, width = w_out.shape
    share = rows // parts
    pieces = lax.all_to_all(w_out.reshape(parts, share, width), "tp", 0, 0, tiled=True)
    mine = jnp.transpose(pieces, (1, 0, 2)).reshape(share, parts * width)
    padded = -(-share // 8) * 8
    mine = jnp.pad(mine, ((0, padded - share), (0, 0)))
    return lax.all_gather(mine, "req", axis=0, tiled=True), share


def shards(q_new, k_new, v_new, k_cache, v_cache, lengths, page_table, w_out):
    own_rows = q_new.shape[0]
    all_rows = 2 * own_rows
    local_heads = k_new.shape[1] // HD
    pages_local = k_cache.shape[0]
    page_rows = k_cache.shape[1]
    block_rows = BLOCK_PAGES * page_rows
    scale = 1.0 / math.sqrt(HD)
    weights_mine, share = output_rows(w_out)
    device_row = lax.axis_index("req")
    parity = device_row % 2
    request = device_row // 2
    length = lengths[request]
    own_places = length + parity * own_rows + jnp.arange(own_rows)
    own_queries = rotate(
        q_new.reshape(own_rows, local_heads * GROUP, HD).astype(jnp.float32), own_places
    ).astype(jnp.bfloat16)
    own_keys = rotate(
        k_new.reshape(own_rows, local_heads, HD).astype(jnp.float32), own_places
    ).astype(jnp.bfloat16)
    own_values = v_new.reshape(own_rows, local_heads, HD)
    peer_queries, peer_keys, peer_values = from_partner(
        (own_queries, own_keys, own_values), "req", 0
    )

    def ordered(mine, theirs):
        return jnp.where(
            parity == 0,
            jnp.concatenate([mine, theirs], axis=0),
            jnp.concatenate([theirs, mine], axis=0),
        )

    queries = ordered(own_queries, peer_queries).reshape(all_rows, local_heads, GROUP, HD)
    fresh_keys = ordered(own_keys, peer_keys)
    fresh_values = ordered(own_values, peer_values)
    state = (
        jnp.full((local_heads, GROUP, all_rows), FLOOR_SCORE, jnp.float32),
        jnp.zeros((local_heads, GROUP, all_rows), jnp.float32),
        jnp.zeros((all_rows, local_heads, GROUP, HD), jnp.float32),
    )
    token_index = jnp.arange(all_rows)
    causal = (token_index[None, :] <= token_index[:, None]) & (parity == 1)
    state = absorb(state, queries, fresh_keys, fresh_values, causal, scale)
    page_count = (length + page_rows - 1) // page_rows
    even_pages = (page_count + 1) // 2
    first_page = jnp.where(parity == 0, 0, even_pages)
    last_page = jnp.where(parity == 0, even_pages, page_count)
    table_row = jnp.concatenate([page_table[request], jnp.full((BLOCK_PAGES,), -1, jnp.int32)])
    offset = device_row * pages_local
    block_count = (last_page - first_page + BLOCK_PAGES - 1) // BLOCK_PAGES

    def visit(block, carry):
        block_first = first_page + block * BLOCK_PAGES
        logical = block_first + jnp.arange(BLOCK_PAGES)
        physical = lax.dynamic_slice(table_row, (block_first,), (BLOCK_PAGES,))
        slots = jnp.clip(physical - offset, 0, pages_local - 1)
        block_keys = k_cache[slots].reshape(block_rows, local_heads, HD)
        block_values = v_cache[slots].reshape(block_rows, local_heads, HD)
        key_places = (logical[:, None] * page_rows + jnp.arange(page_rows)[None, :]).reshape(
            block_rows
        )
        usable = jnp.repeat(logical < last_page, page_rows) & (key_places < length)
        allowed = jnp.broadcast_to(usable[None, :], (all_rows, block_rows))
        return absorb(carry, queries, block_keys, block_values, allowed, scale)

    running_max, running_sum, output = lax.fori_loop(0, block_count, visit, state)
    peer_start = (1 - parity) * own_rows
    own_start = parity * own_rows
    outgoing = (
        lax.dynamic_slice_in_dim(output, peer_start, own_rows, 0),
        lax.dynamic_slice_in_dim(running_max, peer_start, own_rows, 2),
        lax.dynamic_slice_in_dim(running_sum, peer_start, own_rows, 2),
    )
    other_output, other_max, other_sum = (
        from_partner(outgoing[0].astype(jnp.bfloat16), "req", 0).astype(jnp.float32),
        from_partner(outgoing[1].astype(jnp.bfloat16), "req", 0).astype(jnp.float32),
        from_partner(outgoing[2].astype(jnp.bfloat16), "req", 0).astype(jnp.float32),
    )
    mine_output = lax.dynamic_slice_in_dim(output, own_start, own_rows, 0)
    mine_max = lax.dynamic_slice_in_dim(running_max, own_start, own_rows, 2)
    mine_sum = lax.dynamic_slice_in_dim(running_sum, own_start, own_rows, 2)
    joint_max = jnp.maximum(mine_max, other_max)
    mine_factor = jnp.exp(mine_max - joint_max)
    other_factor = jnp.exp(other_max - joint_max)
    joint_sum = mine_sum * mine_factor + other_sum * other_factor
    joint_output = (
        mine_output * jnp.transpose(mine_factor, (2, 0, 1))[..., None]
        + other_output * jnp.transpose(other_factor, (2, 0, 1))[..., None]
    )
    attention = (
        (joint_output / jnp.transpose(joint_sum, (2, 0, 1))[..., None])
        .reshape(own_rows, local_heads * GROUP * HD)
        .astype(jnp.bfloat16)
    )
    full_rows = lax.all_gather(attention, "tp", axis=1, tiled=True)
    projected = lax.dot_general(
        full_rows,
        weights_mine,
        (((1,), (1,)), ((), ())),
        preferred_element_type=jnp.float32,
    )
    blocks = weights_mine.shape[0] // (-(-share // 8) * 8)
    projected = projected.reshape(own_rows, blocks, -1)[:, :, :share].astype(jnp.bfloat16)
    gathered = lax.all_gather(projected, "tp", axis=2, tiled=True)
    return gathered.reshape(own_rows, -1)


def solution(mesh):
    in_specs = (
        P("req", "tp"),
        P("req", "tp"),
        P("req", "tp"),
        P("req", None, "tp"),
        P("req", None, "tp"),
        P(),
        P(),
        P("req", "tp"),
    )
    out_specs = P("req", None)
    return jax.shard_map(shards, mesh=mesh, in_specs=in_specs, out_specs=out_specs, check_vma=False)
```

```python
import math

import jax
import jax.numpy as jnp
from jax import lax
from jax.sharding import PartitionSpec as P

HD = 128
GROUP = 5
BLOCK_PAGES = 4


ROPE_BASE = 1000000.0
FLOOR_SCORE = -1e30


def from_partner(value, axis, distance):
    return lax.ppermute(value, axis, [(i, i ^ 1 << distance) for i in range(lax.axis_size(axis))])


def from_tp(value, shift):
    if shift == 0:
        return value
    size = lax.axis_size("tp")
    return lax.ppermute(value, "tp", [(i, (i + shift) % size) for i in range(size)])


def rotate(values, places):
    inverse = 1.0 / ROPE_BASE ** (jnp.arange(0, HD, 2).astype(jnp.float32) / HD)
    angles = places.astype(jnp.float32)[:, None] * inverse[None, :]
    cosine = jnp.concatenate([jnp.cos(angles), jnp.cos(angles)], axis=-1)[:, None, :]
    sine = jnp.concatenate([jnp.sin(angles), jnp.sin(angles)], axis=-1)[:, None, :]
    first_half = values[..., : HD // 2]
    second_half = values[..., HD // 2 :]
    turned = jnp.concatenate([-second_half, first_half], axis=-1)
    return values * cosine + turned * sine


def absorb(state, queries, block_keys, block_values, allowed, scale):
    running_max, running_sum, output = state
    scores = (
        jnp.einsum("qcgd,kcd->cgqk", queries, block_keys, preferred_element_type=jnp.float32)
        * scale
    )
    scores = jnp.where(allowed[None, None], scores, FLOOR_SCORE)
    new_max = jnp.maximum(running_max, jnp.max(scores, axis=-1))
    factor = jnp.exp(running_max - new_max)
    weights = jnp.where(allowed[None, None], jnp.exp(scores - new_max[..., None]), 0.0)
    running_sum = running_sum * factor + jnp.sum(weights, axis=-1)
    mixed = jnp.einsum(
        "cgqk,kcd->qcgd",
        weights.astype(jnp.bfloat16),
        block_values,
        preferred_element_type=jnp.float32,
    )
    output = output * jnp.transpose(factor, (2, 0, 1))[..., None] + mixed
    return (new_max, running_sum, output)


def output_rows(w_out):
    parts = lax.axis_size("tp")
    rows, width = w_out.shape
    share = rows // parts
    pieces = lax.all_to_all(w_out.reshape(parts, share, width), "tp", 0, 0, tiled=True)
    mine = jnp.transpose(pieces, (1, 0, 2)).reshape(share, parts * width)
    padded = -(-share // 8) * 8
    mine = jnp.pad(mine, ((0, padded - share), (0, 0)))
    return lax.all_gather(mine, "req", axis=0, tiled=True), share


def shards(q_new, k_new, v_new, k_cache, v_cache, lengths, page_table, w_out):
    own_rows = q_new.shape[0]
    all_rows = 2 * own_rows
    local_heads = k_new.shape[1] // HD
    pages_local = k_cache.shape[0]
    page_rows = k_cache.shape[1]
    block_rows = BLOCK_PAGES * page_rows
    scale = 1.0 / math.sqrt(HD)
    weights_mine, share = output_rows(w_out)
    device_row = lax.axis_index("req")
    parity = device_row % 2
    request = device_row // 2
    length = lengths[request]
    own_places = length + parity * own_rows + jnp.arange(own_rows)
    own_queries = rotate(
        q_new.reshape(own_rows, local_heads * GROUP, HD).astype(jnp.float32), own_places
    ).astype(jnp.bfloat16)
    own_keys = rotate(
        k_new.reshape(own_rows, local_heads, HD).astype(jnp.float32), own_places
    ).astype(jnp.bfloat16)
    own_values = v_new.reshape(own_rows, local_heads, HD)
    peer_queries, peer_keys, peer_values = from_partner(
        (own_queries, own_keys, own_values), "req", 0
    )

    def ordered(mine, theirs):
        return jnp.where(
            parity == 0,
            jnp.concatenate([mine, theirs], axis=0),
            jnp.concatenate([theirs, mine], axis=0),
        )

    queries = ordered(own_queries, peer_queries).reshape(all_rows, local_heads, GROUP, HD)
    fresh_keys = ordered(own_keys, peer_keys)
    fresh_values = ordered(own_values, peer_values)
    state = (
        jnp.full((local_heads, GROUP, all_rows), FLOOR_SCORE, jnp.float32),
        jnp.zeros((local_heads, GROUP, all_rows), jnp.float32),
        jnp.zeros((all_rows, local_heads, GROUP, HD), jnp.float32),
    )
    token_index = jnp.arange(all_rows)
    causal = (token_index[None, :] <= token_index[:, None]) & (parity == 1)
    state = absorb(state, queries, fresh_keys, fresh_values, causal, scale)
    page_count = (length + page_rows - 1) // page_rows
    even_pages = (page_count + 1) // 2
    first_page = jnp.where(parity == 0, 0, even_pages)
    last_page = jnp.where(parity == 0, even_pages, page_count)
    table_row = jnp.concatenate([page_table[request], jnp.full((BLOCK_PAGES,), -1, jnp.int32)])
    offset = device_row * pages_local
    block_count = (last_page - first_page + BLOCK_PAGES - 1) // BLOCK_PAGES

    def visit(block, carry):
        block_first = first_page + block * BLOCK_PAGES
        logical = block_first + jnp.arange(BLOCK_PAGES)
        physical = lax.dynamic_slice(table_row, (block_first,), (BLOCK_PAGES,))
        slots = jnp.clip(physical - offset, 0, pages_local - 1)
        block_keys = k_cache[slots].reshape(block_rows, local_heads, HD)
        block_values = v_cache[slots].reshape(block_rows, local_heads, HD)
        key_places = (logical[:, None] * page_rows + jnp.arange(page_rows)[None, :]).reshape(
            block_rows
        )
        usable = jnp.repeat(logical < last_page, page_rows) & (key_places < length)
        allowed = jnp.broadcast_to(usable[None, :], (all_rows, block_rows))
        return absorb(carry, queries, block_keys, block_values, allowed, scale)

    running_max, running_sum, output = lax.fori_loop(0, block_count, visit, state)
    peer_start = (1 - parity) * own_rows
    own_start = parity * own_rows
    outgoing = (
        lax.dynamic_slice_in_dim(output, peer_start, own_rows, 0),
        lax.dynamic_slice_in_dim(running_max, peer_start, own_rows, 2),
        lax.dynamic_slice_in_dim(running_sum, peer_start, own_rows, 2),
    )
    other_output, other_max, other_sum = (
        from_partner(outgoing[0].astype(jnp.bfloat16), "req", 0).astype(jnp.float32),
        from_partner(outgoing[1].astype(jnp.bfloat16), "req", 0).astype(jnp.float32),
        from_partner(outgoing[2].astype(jnp.bfloat16), "req", 0).astype(jnp.float32),
    )
    mine_output = lax.dynamic_slice_in_dim(output, own_start, own_rows, 0)
    mine_max = lax.dynamic_slice_in_dim(running_max, own_start, own_rows, 2)
    mine_sum = lax.dynamic_slice_in_dim(running_sum, own_start, own_rows, 2)
    joint_max = jnp.maximum(mine_max, other_max)
    mine_factor = jnp.exp(mine_max - joint_max)
    other_factor = jnp.exp(other_max - joint_max)
    joint_sum = mine_sum * mine_factor + other_sum * other_factor
    joint_output = (
        mine_output * jnp.transpose(mine_factor, (2, 0, 1))[..., None]
        + other_output * jnp.transpose(other_factor, (2, 0, 1))[..., None]
    )
    attention = (
        (joint_output / jnp.transpose(joint_sum, (2, 0, 1))[..., None])
        .reshape(own_rows, local_heads * GROUP * HD)
        .astype(jnp.bfloat16)
    )
    parts = lax.axis_size("tp")
    full_rows = lax.all_gather(attention, "tp", axis=1, tiled=True)
    projected = lax.dot_general(
        full_rows,
        weights_mine,
        (((1,), (1,)), ((), ())),
        preferred_element_type=jnp.float32,
    )
    blocks = weights_mine.shape[0] // (-(-share // 8) * 8)
    projected = projected.reshape(own_rows, blocks, -1)[:, :, :share].astype(jnp.bfloat16)
    gathered = jnp.stack([from_tp(projected, shift) for shift in range(parts)])
    sources = (lax.axis_index("tp") - jnp.arange(parts)) % parts
    gathered = jnp.take(gathered, sources, axis=0)
    return jnp.transpose(gathered, (1, 2, 0, 3)).reshape(own_rows, -1)


def solution(mesh):
    in_specs = (
        P("req", "tp"),
        P("req", "tp"),
        P("req", "tp"),
        P("req", None, "tp"),
        P("req", None, "tp"),
        P(),
        P(),
        P("req", "tp"),
    )
    out_specs = P("req", None)
    return jax.shard_map(shards, mesh=mesh, in_specs=in_specs, out_specs=out_specs, check_vma=False)
```

```python
import math

import jax
import jax.numpy as jnp
from jax import lax
from jax.sharding import PartitionSpec as P

HD = 128
GROUP = 5
BLOCK_PAGES = 4


ROPE_BASE = 1000000.0
FLOOR_SCORE = -1e30


def from_partner(value, axis, distance):
    return lax.ppermute(value, axis, [(i, i ^ 1 << distance) for i in range(lax.axis_size(axis))])


def rotate(values, places):
    inverse = 1.0 / ROPE_BASE ** (jnp.arange(0, HD, 2).astype(jnp.float32) / HD)
    angles = places.astype(jnp.float32)[:, None] * inverse[None, :]
    cosine = jnp.concatenate([jnp.cos(angles), jnp.cos(angles)], axis=-1)[:, None, :]
    sine = jnp.concatenate([jnp.sin(angles), jnp.sin(angles)], axis=-1)[:, None, :]
    first_half = values[..., : HD // 2]
    second_half = values[..., HD // 2 :]
    turned = jnp.concatenate([-second_half, first_half], axis=-1)
    return values * cosine + turned * sine


def absorb(state, queries, block_keys, block_values, allowed, scale):
    running_max, running_sum, output = state
    scores = (
        jnp.einsum("qcgd,kcd->cgqk", queries, block_keys, preferred_element_type=jnp.float32)
        * scale
    )
    scores = jnp.where(allowed[None, None], scores, FLOOR_SCORE)
    new_max = jnp.maximum(running_max, jnp.max(scores, axis=-1))
    factor = jnp.exp(running_max - new_max)
    weights = jnp.where(allowed[None, None], jnp.exp(scores - new_max[..., None]), 0.0)
    running_sum = running_sum * factor + jnp.sum(weights, axis=-1)
    mixed = jnp.einsum(
        "cgqk,kcd->qcgd",
        weights.astype(jnp.bfloat16),
        block_values,
        preferred_element_type=jnp.float32,
    )
    output = output * jnp.transpose(factor, (2, 0, 1))[..., None] + mixed
    return (new_max, running_sum, output)


def output_rows(w_out):
    parts = lax.axis_size("tp")
    rows, width = w_out.shape
    share = rows // parts
    pieces = lax.all_to_all(w_out.reshape(parts, share, width), "tp", 0, 0, tiled=True)
    mine = jnp.transpose(pieces, (1, 0, 2)).reshape(share, parts * width)
    padded = -(-share // 8) * 8
    mine = jnp.pad(mine, ((0, padded - share), (0, 0)))
    return lax.all_gather(mine, "req", axis=0, tiled=True), share


def shards(q_new, k_new, v_new, k_cache, v_cache, lengths, page_table, w_out):
    own_rows = q_new.shape[0]
    all_rows = 2 * own_rows
    local_heads = k_new.shape[1] // HD
    pages_local = k_cache.shape[0]
    page_rows = k_cache.shape[1]
    block_rows = BLOCK_PAGES * page_rows
    scale = 1.0 / math.sqrt(HD)
    weights_mine, share = output_rows(w_out)
    device_row = lax.axis_index("req")
    parity = device_row % 2
    request = device_row // 2
    length = lengths[request]
    own_places = length + parity * own_rows + jnp.arange(own_rows)
    own_queries = rotate(
        q_new.reshape(own_rows, local_heads * GROUP, HD).astype(jnp.float32), own_places
    ).astype(jnp.bfloat16)
    own_keys = rotate(
        k_new.reshape(own_rows, local_heads, HD).astype(jnp.float32), own_places
    ).astype(jnp.bfloat16)
    own_values = v_new.reshape(own_rows, local_heads, HD)
    peer_queries, peer_keys, peer_values = from_partner(
        (own_queries, own_keys, own_values), "req", 0
    )

    def ordered(mine, theirs):
        return jnp.where(
            parity == 0,
            jnp.concatenate([mine, theirs], axis=0),
            jnp.concatenate([theirs, mine], axis=0),
        )

    queries = ordered(own_queries, peer_queries).reshape(all_rows, local_heads, GROUP, HD)
    fresh_keys = ordered(own_keys, peer_keys)
    fresh_values = ordered(own_values, peer_values)
    state = (
        jnp.full((local_heads, GROUP, all_rows), FLOOR_SCORE, jnp.float32),
        jnp.zeros((local_heads, GROUP, all_rows), jnp.float32),
        jnp.zeros((all_rows, local_heads, GROUP, HD), jnp.float32),
    )
    token_index = jnp.arange(all_rows)
    causal = (token_index[None, :] <= token_index[:, None]) & (parity == 1)
    state = absorb(state, queries, fresh_keys, fresh_values, causal, scale)
    page_count = (length + page_rows - 1) // page_rows
    even_pages = (page_count + 1) // 2
    first_page = jnp.where(parity == 0, 0, even_pages)
    last_page = jnp.where(parity == 0, even_pages, page_count)
    table_row = jnp.concatenate([page_table[request], jnp.full((BLOCK_PAGES,), -1, jnp.int32)])
    offset = device_row * pages_local
    block_count = (last_page - first_page + BLOCK_PAGES - 1) // BLOCK_PAGES

    def visit(block, carry):
        block_first = first_page + block * BLOCK_PAGES
        logical = block_first + jnp.arange(BLOCK_PAGES)
        physical = lax.dynamic_slice(table_row, (block_first,), (BLOCK_PAGES,))
        slots = jnp.clip(physical - offset, 0, pages_local - 1)
        block_keys = k_cache[slots].reshape(block_rows, local_heads, HD)
        block_values = v_cache[slots].reshape(block_rows, local_heads, HD)
        key_places = (logical[:, None] * page_rows + jnp.arange(page_rows)[None, :]).reshape(
            block_rows
        )
        usable = jnp.repeat(logical < last_page, page_rows) & (key_places < length)
        allowed = jnp.broadcast_to(usable[None, :], (all_rows, block_rows))
        return absorb(carry, queries, block_keys, block_values, allowed, scale)

    running_max, running_sum, output = lax.fori_loop(0, block_count, visit, state)
    peer_start = (1 - parity) * own_rows
    own_start = parity * own_rows
    outgoing = (
        lax.dynamic_slice_in_dim(output, peer_start, own_rows, 0),
        lax.dynamic_slice_in_dim(running_max, peer_start, own_rows, 2),
        lax.dynamic_slice_in_dim(running_sum, peer_start, own_rows, 2),
    )
    other_output, other_max, other_sum = (
        from_partner(outgoing[0].astype(jnp.bfloat16), "req", 0).astype(jnp.float32),
        from_partner(outgoing[1].astype(jnp.bfloat16), "req", 0).astype(jnp.float32),
        from_partner(outgoing[2].astype(jnp.bfloat16), "req", 0).astype(jnp.float32),
    )
    mine_output = lax.dynamic_slice_in_dim(output, own_start, own_rows, 0)
    mine_max = lax.dynamic_slice_in_dim(running_max, own_start, own_rows, 2)
    mine_sum = lax.dynamic_slice_in_dim(running_sum, own_start, own_rows, 2)
    joint_max = jnp.maximum(mine_max, other_max)
    mine_factor = jnp.exp(mine_max - joint_max)
    other_factor = jnp.exp(other_max - joint_max)
    joint_sum = mine_sum * mine_factor + other_sum * other_factor
    joint_output = (
        mine_output * jnp.transpose(mine_factor, (2, 0, 1))[..., None]
        + other_output * jnp.transpose(other_factor, (2, 0, 1))[..., None]
    )
    attention = (
        (joint_output / jnp.transpose(joint_sum, (2, 0, 1))[..., None])
        .reshape(own_rows, local_heads * GROUP * HD)
        .astype(jnp.bfloat16)
    )
    full_rows = lax.all_gather(attention, "tp", axis=1, tiled=True)
    projected = lax.dot_general(
        full_rows,
        weights_mine,
        (((1,), (1,)), ((), ())),
        preferred_element_type=jnp.float32,
    )
    blocks = weights_mine.shape[0] // (-(-share // 8) * 8)
    projected = projected.reshape(own_rows, blocks, -1)[:, :, :share].astype(jnp.bfloat16)
    parts = lax.axis_size("tp")
    rows, blocks, share = projected.shape
    copies = jnp.broadcast_to(projected[:, :, None], (rows, blocks, parts, share))
    gathered = lax.all_to_all(copies, "tp", 2, 2, tiled=True)
    return gathered.reshape(own_rows, -1)


def solution(mesh):
    in_specs = (
        P("req", "tp"),
        P("req", "tp"),
        P("req", "tp"),
        P("req", None, "tp"),
        P("req", None, "tp"),
        P(),
        P(),
        P("req", "tp"),
    )
    out_specs = P("req", None)
    return jax.shard_map(shards, mesh=mesh, in_specs=in_specs, out_specs=out_specs, check_vma=False)
```

```python
import math

import jax
import jax.numpy as jnp
from jax import lax
from jax.sharding import PartitionSpec as P

HD = 128
GROUP = 5
BLOCK_PAGES = 4


ROPE_BASE = 1000000.0
FLOOR_SCORE = -1e30


def from_partner(value, axis, distance):
    return lax.ppermute(value, axis, [(i, i ^ 1 << distance) for i in range(lax.axis_size(axis))])


def rotate(values, places):
    inverse = 1.0 / ROPE_BASE ** (jnp.arange(0, HD, 2).astype(jnp.float32) / HD)
    angles = places.astype(jnp.float32)[:, None] * inverse[None, :]
    cosine = jnp.concatenate([jnp.cos(angles), jnp.cos(angles)], axis=-1)[:, None, :]
    sine = jnp.concatenate([jnp.sin(angles), jnp.sin(angles)], axis=-1)[:, None, :]
    first_half = values[..., : HD // 2]
    second_half = values[..., HD // 2 :]
    turned = jnp.concatenate([-second_half, first_half], axis=-1)
    return values * cosine + turned * sine


def absorb(state, queries, block_keys, block_values, allowed, scale):
    running_max, running_sum, output = state
    scores = (
        jnp.einsum("qcgd,kcd->cgqk", queries, block_keys, preferred_element_type=jnp.float32)
        * scale
    )
    scores = jnp.where(allowed[None, None], scores, FLOOR_SCORE)
    new_max = jnp.maximum(running_max, jnp.max(scores, axis=-1))
    factor = jnp.exp(running_max - new_max)
    weights = jnp.where(allowed[None, None], jnp.exp(scores - new_max[..., None]), 0.0)
    running_sum = running_sum * factor + jnp.sum(weights, axis=-1)
    mixed = jnp.einsum(
        "cgqk,kcd->qcgd",
        weights.astype(jnp.bfloat16),
        block_values,
        preferred_element_type=jnp.float32,
    )
    output = output * jnp.transpose(factor, (2, 0, 1))[..., None] + mixed
    return (new_max, running_sum, output)


def output_rows(w_out):
    parts = lax.axis_size("tp")
    rows, width = w_out.shape
    share = rows // parts
    pieces = lax.all_to_all(w_out.reshape(parts, share, width), "tp", 0, 0, tiled=True)
    mine = jnp.transpose(pieces, (1, 0, 2))
    return lax.all_gather(mine, "req", axis=0, tiled=True), share


def shards(q_new, k_new, v_new, k_cache, v_cache, lengths, page_table, w_out):
    own_rows = q_new.shape[0]
    all_rows = 2 * own_rows
    local_heads = k_new.shape[1] // HD
    pages_local = k_cache.shape[0]
    page_rows = k_cache.shape[1]
    block_rows = BLOCK_PAGES * page_rows
    scale = 1.0 / math.sqrt(HD)
    weights_mine, share = output_rows(w_out)
    device_row = lax.axis_index("req")
    parity = device_row % 2
    request = device_row // 2
    length = lengths[request]
    own_places = length + parity * own_rows + jnp.arange(own_rows)
    own_queries = rotate(
        q_new.reshape(own_rows, local_heads * GROUP, HD).astype(jnp.float32), own_places
    ).astype(jnp.bfloat16)
    own_keys = rotate(
        k_new.reshape(own_rows, local_heads, HD).astype(jnp.float32), own_places
    ).astype(jnp.bfloat16)
    own_values = v_new.reshape(own_rows, local_heads, HD)
    peer_queries, peer_keys, peer_values = from_partner(
        (own_queries, own_keys, own_values), "req", 0
    )

    def ordered(mine, theirs):
        return jnp.where(
            parity == 0,
            jnp.concatenate([mine, theirs], axis=0),
            jnp.concatenate([theirs, mine], axis=0),
        )

    queries = ordered(own_queries, peer_queries).reshape(all_rows, local_heads, GROUP, HD)
    fresh_keys = ordered(own_keys, peer_keys)
    fresh_values = ordered(own_values, peer_values)
    state = (
        jnp.full((local_heads, GROUP, all_rows), FLOOR_SCORE, jnp.float32),
        jnp.zeros((local_heads, GROUP, all_rows), jnp.float32),
        jnp.zeros((all_rows, local_heads, GROUP, HD), jnp.float32),
    )
    token_index = jnp.arange(all_rows)
    causal = (token_index[None, :] <= token_index[:, None]) & (parity == 1)
    state = absorb(state, queries, fresh_keys, fresh_values, causal, scale)
    page_count = (length + page_rows - 1) // page_rows
    even_pages = (page_count + 1) // 2
    first_page = jnp.where(parity == 0, 0, even_pages)
    last_page = jnp.where(parity == 0, even_pages, page_count)
    table_row = jnp.concatenate([page_table[request], jnp.full((BLOCK_PAGES,), -1, jnp.int32)])
    offset = device_row * pages_local
    block_count = (last_page - first_page + BLOCK_PAGES - 1) // BLOCK_PAGES

    def visit(block, carry):
        block_first = first_page + block * BLOCK_PAGES
        logical = block_first + jnp.arange(BLOCK_PAGES)
        physical = lax.dynamic_slice(table_row, (block_first,), (BLOCK_PAGES,))
        slots = jnp.clip(physical - offset, 0, pages_local - 1)
        block_keys = k_cache[slots].reshape(block_rows, local_heads, HD)
        block_values = v_cache[slots].reshape(block_rows, local_heads, HD)
        key_places = (logical[:, None] * page_rows + jnp.arange(page_rows)[None, :]).reshape(
            block_rows
        )
        usable = jnp.repeat(logical < last_page, page_rows) & (key_places < length)
        allowed = jnp.broadcast_to(usable[None, :], (all_rows, block_rows))
        return absorb(carry, queries, block_keys, block_values, allowed, scale)

    running_max, running_sum, output = lax.fori_loop(0, block_count, visit, state)
    peer_start = (1 - parity) * own_rows
    own_start = parity * own_rows
    outgoing = (
        lax.dynamic_slice_in_dim(output, peer_start, own_rows, 0),
        lax.dynamic_slice_in_dim(running_max, peer_start, own_rows, 2),
        lax.dynamic_slice_in_dim(running_sum, peer_start, own_rows, 2),
    )
    other_output, other_max, other_sum = (
        from_partner(outgoing[0].astype(jnp.bfloat16), "req", 0).astype(jnp.float32),
        from_partner(outgoing[1].astype(jnp.bfloat16), "req", 0).astype(jnp.float32),
        from_partner(outgoing[2].astype(jnp.bfloat16), "req", 0).astype(jnp.float32),
    )
    mine_output = lax.dynamic_slice_in_dim(output, own_start, own_rows, 0)
    mine_max = lax.dynamic_slice_in_dim(running_max, own_start, own_rows, 2)
    mine_sum = lax.dynamic_slice_in_dim(running_sum, own_start, own_rows, 2)
    joint_max = jnp.maximum(mine_max, other_max)
    mine_factor = jnp.exp(mine_max - joint_max)
    other_factor = jnp.exp(other_max - joint_max)
    joint_sum = mine_sum * mine_factor + other_sum * other_factor
    joint_output = (
        mine_output * jnp.transpose(mine_factor, (2, 0, 1))[..., None]
        + other_output * jnp.transpose(other_factor, (2, 0, 1))[..., None]
    )
    attention = (
        (joint_output / jnp.transpose(joint_sum, (2, 0, 1))[..., None])
        .reshape(own_rows, local_heads * GROUP * HD)
        .astype(jnp.bfloat16)
    )
    full_rows = lax.all_gather(attention[:, None], "tp", axis=1, tiled=True)
    projected = lax.dot_general(
        full_rows,
        weights_mine,
        (((1, 2), (1, 2)), ((), ())),
        preferred_element_type=jnp.float32,
    )
    projected = projected.reshape(own_rows, -1, share).astype(jnp.bfloat16)
    gathered = lax.all_gather(projected, "tp", axis=2, tiled=True)
    return gathered.reshape(own_rows, -1)


def solution(mesh):
    in_specs = (
        P("req", "tp"),
        P("req", "tp"),
        P("req", "tp"),
        P("req", None, "tp"),
        P("req", None, "tp"),
        P(),
        P(),
        P("req", "tp"),
    )
    out_specs = P("req", None)
    return jax.shard_map(shards, mesh=mesh, in_specs=in_specs, out_specs=out_specs, check_vma=False)
```

```python
import math

import jax
import jax.numpy as jnp
from jax import lax
from jax.sharding import Mesh
from jax.sharding import PartitionSpec as P

HD = 128
GROUP = 5
BLOCK_PAGES = 4
ROWS = ("z", "x", "core")


ROPE_BASE = 1000000.0
FLOOR_SCORE = -1e30


def from_partner(value, axis, distance):
    return lax.ppermute(value, axis, [(i, i ^ 1 << distance) for i in range(lax.axis_size(axis))])


def rotate(values, places):
    inverse = 1.0 / ROPE_BASE ** (jnp.arange(0, HD, 2).astype(jnp.float32) / HD)
    angles = places.astype(jnp.float32)[:, None] * inverse[None, :]
    cosine = jnp.concatenate([jnp.cos(angles), jnp.cos(angles)], axis=-1)[:, None, :]
    sine = jnp.concatenate([jnp.sin(angles), jnp.sin(angles)], axis=-1)[:, None, :]
    first_half = values[..., : HD // 2]
    second_half = values[..., HD // 2 :]
    turned = jnp.concatenate([-second_half, first_half], axis=-1)
    return values * cosine + turned * sine


def absorb(state, queries, block_keys, block_values, allowed, scale):
    running_max, running_sum, output = state
    scores = (
        jnp.einsum("qcgd,kcd->cgqk", queries, block_keys, preferred_element_type=jnp.float32)
        * scale
    )
    scores = jnp.where(allowed[None, None], scores, FLOOR_SCORE)
    new_max = jnp.maximum(running_max, jnp.max(scores, axis=-1))
    factor = jnp.exp(running_max - new_max)
    weights = jnp.where(allowed[None, None], jnp.exp(scores - new_max[..., None]), 0.0)
    running_sum = running_sum * factor + jnp.sum(weights, axis=-1)
    mixed = jnp.einsum(
        "cgqk,kcd->qcgd",
        weights.astype(jnp.bfloat16),
        block_values,
        preferred_element_type=jnp.float32,
    )
    output = output * jnp.transpose(factor, (2, 0, 1))[..., None] + mixed
    return (new_max, running_sum, output)


def output_rows(w_out):
    parts = lax.axis_size("tp")
    rows, width = w_out.shape
    share = rows // parts
    pieces = lax.all_to_all(w_out.reshape(parts, share, width), "tp", 0, 0, tiled=True)
    mine = jnp.transpose(pieces, (1, 0, 2))
    near = lax.all_gather(mine, "z", axis=0, tiled=True)
    return lax.all_gather(near, ("x", "core"), axis=0, tiled=True), share


def shards(q_new, k_new, v_new, k_cache, v_cache, lengths, page_table, w_out):
    own_rows = q_new.shape[0]
    all_rows = 2 * own_rows
    local_heads = k_new.shape[1] // HD
    pages_local = k_cache.shape[0]
    page_rows = k_cache.shape[1]
    block_rows = BLOCK_PAGES * page_rows
    scale = 1.0 / math.sqrt(HD)
    weights_mine, share = output_rows(w_out)
    device_row = (lax.axis_index("z") * lax.axis_size("x") + lax.axis_index("x")) * lax.axis_size(
        "core"
    ) + lax.axis_index("core")
    parity = device_row % 2
    request = device_row // 2
    length = lengths[request]
    own_places = length + parity * own_rows + jnp.arange(own_rows)
    own_queries = rotate(
        q_new.reshape(own_rows, local_heads * GROUP, HD).astype(jnp.float32), own_places
    ).astype(jnp.bfloat16)
    own_keys = rotate(
        k_new.reshape(own_rows, local_heads, HD).astype(jnp.float32), own_places
    ).astype(jnp.bfloat16)
    own_values = v_new.reshape(own_rows, local_heads, HD)
    peer_queries, peer_keys, peer_values = from_partner(
        (own_queries, own_keys, own_values), "core", 0
    )

    def ordered(mine, theirs):
        return jnp.where(
            parity == 0,
            jnp.concatenate([mine, theirs], axis=0),
            jnp.concatenate([theirs, mine], axis=0),
        )

    queries = ordered(own_queries, peer_queries).reshape(all_rows, local_heads, GROUP, HD)
    fresh_keys = ordered(own_keys, peer_keys)
    fresh_values = ordered(own_values, peer_values)
    state = (
        jnp.full((local_heads, GROUP, all_rows), FLOOR_SCORE, jnp.float32),
        jnp.zeros((local_heads, GROUP, all_rows), jnp.float32),
        jnp.zeros((all_rows, local_heads, GROUP, HD), jnp.float32),
    )
    token_index = jnp.arange(all_rows)
    causal = (token_index[None, :] <= token_index[:, None]) & (parity == 1)
    state = absorb(state, queries, fresh_keys, fresh_values, causal, scale)
    page_count = (length + page_rows - 1) // page_rows
    even_pages = (page_count + 1) // 2
    first_page = jnp.where(parity == 0, 0, even_pages)
    last_page = jnp.where(parity == 0, even_pages, page_count)
    table_row = jnp.concatenate([page_table[request], jnp.full((BLOCK_PAGES,), -1, jnp.int32)])
    offset = device_row * pages_local
    block_count = (last_page - first_page + BLOCK_PAGES - 1) // BLOCK_PAGES

    def visit(block, carry):
        block_first = first_page + block * BLOCK_PAGES
        logical = block_first + jnp.arange(BLOCK_PAGES)
        physical = lax.dynamic_slice(table_row, (block_first,), (BLOCK_PAGES,))
        slots = jnp.clip(physical - offset, 0, pages_local - 1)
        block_keys = k_cache[slots].reshape(block_rows, local_heads, HD)
        block_values = v_cache[slots].reshape(block_rows, local_heads, HD)
        key_places = (logical[:, None] * page_rows + jnp.arange(page_rows)[None, :]).reshape(
            block_rows
        )
        usable = jnp.repeat(logical < last_page, page_rows) & (key_places < length)
        allowed = jnp.broadcast_to(usable[None, :], (all_rows, block_rows))
        return absorb(carry, queries, block_keys, block_values, allowed, scale)

    running_max, running_sum, output = lax.fori_loop(0, block_count, visit, state)
    peer_start = (1 - parity) * own_rows
    own_start = parity * own_rows
    outgoing = (
        lax.dynamic_slice_in_dim(output, peer_start, own_rows, 0),
        lax.dynamic_slice_in_dim(running_max, peer_start, own_rows, 2),
        lax.dynamic_slice_in_dim(running_sum, peer_start, own_rows, 2),
    )
    other_output, other_max, other_sum = (
        from_partner(outgoing[0].astype(jnp.bfloat16), "core", 0).astype(jnp.float32),
        from_partner(outgoing[1].astype(jnp.bfloat16), "core", 0).astype(jnp.float32),
        from_partner(outgoing[2].astype(jnp.bfloat16), "core", 0).astype(jnp.float32),
    )
    mine_output = lax.dynamic_slice_in_dim(output, own_start, own_rows, 0)
    mine_max = lax.dynamic_slice_in_dim(running_max, own_start, own_rows, 2)
    mine_sum = lax.dynamic_slice_in_dim(running_sum, own_start, own_rows, 2)
    joint_max = jnp.maximum(mine_max, other_max)
    mine_factor = jnp.exp(mine_max - joint_max)
    other_factor = jnp.exp(other_max - joint_max)
    joint_sum = mine_sum * mine_factor + other_sum * other_factor
    joint_output = (
        mine_output * jnp.transpose(mine_factor, (2, 0, 1))[..., None]
        + other_output * jnp.transpose(other_factor, (2, 0, 1))[..., None]
    )
    attention = (
        (joint_output / jnp.transpose(joint_sum, (2, 0, 1))[..., None])
        .reshape(own_rows, local_heads * GROUP * HD)
        .astype(jnp.bfloat16)
    )
    full_rows = lax.all_gather(attention[:, None], "tp", axis=1, tiled=True)
    projected = lax.dot_general(
        full_rows,
        weights_mine,
        (((1, 2), (1, 2)), ((), ())),
        preferred_element_type=jnp.float32,
    )
    depth = lax.axis_size("z")
    projected = projected.reshape(own_rows, -1, depth, share)
    projected = jnp.transpose(projected, (0, 2, 1, 3)).reshape(own_rows, -1, share)
    projected = projected.astype(jnp.bfloat16)
    gathered = lax.all_gather(projected, "tp", axis=2, tiled=True)
    return gathered.reshape(own_rows, -1)


def solution(mesh):
    in_specs = (
        P(ROWS, "tp"),
        P(ROWS, "tp"),
        P(ROWS, "tp"),
        P(ROWS, None, "tp"),
        P(ROWS, None, "tp"),
        P(),
        P(),
        P(ROWS, "tp"),
    )
    out_specs = P(ROWS, None)
    rows, parts = mesh.devices.shape
    cores = 2
    depth = 4 if rows % (4 * cores) == 0 else 1
    split = Mesh(mesh.devices.reshape(depth, rows // (depth * cores), cores, parts), ROWS + ("tp",))
    return jax.shard_map(shards, mesh=split, in_specs=in_specs, out_specs=out_specs, check_vma=False)
```

```python
import math

import jax
import jax.numpy as jnp
from jax import lax
from jax.sharding import Mesh
from jax.sharding import PartitionSpec as P

HD = 128
GROUP = 5
ROWS = ("z", "x", "core")


ROPE_BASE = 1000000.0
FLOOR_SCORE = -1e30


def from_partner(value, axis, distance):
    return lax.ppermute(value, axis, [(i, i ^ 1 << distance) for i in range(lax.axis_size(axis))])


def rotate(values, places):
    inverse = 1.0 / ROPE_BASE ** (jnp.arange(0, HD, 2).astype(jnp.float32) / HD)
    angles = places.astype(jnp.float32)[:, None] * inverse[None, :]
    cosine = jnp.concatenate([jnp.cos(angles), jnp.cos(angles)], axis=-1)[:, None, :]
    sine = jnp.concatenate([jnp.sin(angles), jnp.sin(angles)], axis=-1)[:, None, :]
    first_half = values[..., : HD // 2]
    second_half = values[..., HD // 2 :]
    turned = jnp.concatenate([-second_half, first_half], axis=-1)
    return values * cosine + turned * sine


def absorb(state, queries, block_keys, block_values, allowed, scale):
    running_max, running_sum, output = state
    scores = (
        jnp.einsum("qcgd,kcd->cgqk", queries, block_keys, preferred_element_type=jnp.float32)
        * scale
    )
    scores = jnp.where(allowed[None, None], scores, FLOOR_SCORE)
    new_max = jnp.maximum(running_max, jnp.max(scores, axis=-1))
    factor = jnp.exp(running_max - new_max)
    weights = jnp.where(allowed[None, None], jnp.exp(scores - new_max[..., None]), 0.0)
    running_sum = running_sum * factor + jnp.sum(weights, axis=-1)
    mixed = jnp.einsum(
        "cgqk,kcd->qcgd",
        weights.astype(jnp.bfloat16),
        block_values,
        preferred_element_type=jnp.float32,
    )
    output = output * jnp.transpose(factor, (2, 0, 1))[..., None] + mixed
    return (new_max, running_sum, output)


def output_rows(w_out):
    parts = lax.axis_size("tp")
    rows, width = w_out.shape
    share = rows // parts
    pieces = lax.all_to_all(w_out.reshape(parts, share, width), "tp", 0, 0, tiled=True)
    mine = jnp.transpose(pieces, (1, 0, 2))
    near = lax.all_gather(mine, "z", axis=0, tiled=True)
    return lax.all_gather(near, ("x", "core"), axis=0, tiled=True), share


def shards(q_new, k_new, v_new, k_cache, v_cache, lengths, page_table, w_out):
    own_rows = q_new.shape[0]
    all_rows = 2 * own_rows
    local_heads = k_new.shape[1] // HD
    pages_local = k_cache.shape[0]
    page_rows = k_cache.shape[1]
    scale = 1.0 / math.sqrt(HD)
    weights_mine, share = output_rows(w_out)
    device_row = (lax.axis_index("z") * lax.axis_size("x") + lax.axis_index("x")) * lax.axis_size(
        "core"
    ) + lax.axis_index("core")
    parity = device_row % 2
    request = device_row // 2
    length = lengths[request]
    own_places = length + parity * own_rows + jnp.arange(own_rows)
    own_queries = rotate(
        q_new.reshape(own_rows, local_heads * GROUP, HD).astype(jnp.float32), own_places
    ).astype(jnp.bfloat16)
    own_keys = rotate(
        k_new.reshape(own_rows, local_heads, HD).astype(jnp.float32), own_places
    ).astype(jnp.bfloat16)
    own_values = v_new.reshape(own_rows, local_heads, HD)
    peer_queries, peer_keys, peer_values = from_partner(
        (own_queries, own_keys, own_values), "core", 0
    )

    def ordered(mine, theirs):
        return jnp.where(
            parity == 0,
            jnp.concatenate([mine, theirs], axis=0),
            jnp.concatenate([theirs, mine], axis=0),
        )

    queries = ordered(own_queries, peer_queries).reshape(all_rows, local_heads, GROUP, HD)
    fresh_keys = ordered(own_keys, peer_keys)
    fresh_values = ordered(own_values, peer_values)
    state = (
        jnp.full((local_heads, GROUP, all_rows), FLOOR_SCORE, jnp.float32),
        jnp.zeros((local_heads, GROUP, all_rows), jnp.float32),
        jnp.zeros((all_rows, local_heads, GROUP, HD), jnp.float32),
    )
    token_index = jnp.arange(all_rows)
    causal = (token_index[None, :] <= token_index[:, None]) & (parity == 1)
    state = absorb(state, queries, fresh_keys, fresh_values, causal, scale)
    page_count = (length + page_rows - 1) // page_rows
    even_pages = (page_count + 1) // 2
    first_page = jnp.where(parity == 0, 0, even_pages)
    last_page = jnp.where(parity == 0, even_pages, page_count)
    table_row = page_table[request]
    logical = jnp.arange(table_row.shape[0])
    in_range = (logical >= first_page) & (logical < last_page)
    offset = device_row * pages_local
    slot_ids = jnp.arange(pages_local)
    match = in_range[:, None] & (table_row[:, None] - offset == slot_ids[None, :])
    used = jnp.any(match, axis=0)
    base = jnp.sum(jnp.where(match, logical[:, None], 0), axis=0) * page_rows
    key_places = (base[:, None] + jnp.arange(page_rows)[None, :]).reshape(-1)
    usable = jnp.repeat(used, page_rows) & (key_places < length)
    allowed = jnp.broadcast_to(usable[None, :], (all_rows, pages_local * page_rows))
    pool_keys = k_cache.reshape(pages_local * page_rows, local_heads, HD)
    pool_values = v_cache.reshape(pages_local * page_rows, local_heads, HD)
    running_max, running_sum, output = absorb(
        state, queries, pool_keys, pool_values, allowed, scale
    )
    peer_start = (1 - parity) * own_rows
    own_start = parity * own_rows
    outgoing = (
        lax.dynamic_slice_in_dim(output, peer_start, own_rows, 0),
        lax.dynamic_slice_in_dim(running_max, peer_start, own_rows, 2),
        lax.dynamic_slice_in_dim(running_sum, peer_start, own_rows, 2),
    )
    other_output, other_max, other_sum = (
        from_partner(outgoing[0].astype(jnp.bfloat16), "core", 0).astype(jnp.float32),
        from_partner(outgoing[1].astype(jnp.bfloat16), "core", 0).astype(jnp.float32),
        from_partner(outgoing[2].astype(jnp.bfloat16), "core", 0).astype(jnp.float32),
    )
    mine_output = lax.dynamic_slice_in_dim(output, own_start, own_rows, 0)
    mine_max = lax.dynamic_slice_in_dim(running_max, own_start, own_rows, 2)
    mine_sum = lax.dynamic_slice_in_dim(running_sum, own_start, own_rows, 2)
    joint_max = jnp.maximum(mine_max, other_max)
    mine_factor = jnp.exp(mine_max - joint_max)
    other_factor = jnp.exp(other_max - joint_max)
    joint_sum = mine_sum * mine_factor + other_sum * other_factor
    joint_output = (
        mine_output * jnp.transpose(mine_factor, (2, 0, 1))[..., None]
        + other_output * jnp.transpose(other_factor, (2, 0, 1))[..., None]
    )
    attention = (
        (joint_output / jnp.transpose(joint_sum, (2, 0, 1))[..., None])
        .reshape(own_rows, local_heads * GROUP * HD)
        .astype(jnp.bfloat16)
    )
    full_rows = lax.all_gather(attention[:, None], "tp", axis=1, tiled=True)
    projected = lax.dot_general(
        full_rows,
        weights_mine,
        (((1, 2), (1, 2)), ((), ())),
        preferred_element_type=jnp.float32,
    )
    depth = lax.axis_size("z")
    projected = projected.reshape(own_rows, -1, depth, share)
    projected = jnp.transpose(projected, (0, 2, 1, 3)).reshape(own_rows, -1, share)
    projected = projected.astype(jnp.bfloat16)
    gathered = lax.all_gather(projected, "tp", axis=2, tiled=True)
    return gathered.reshape(own_rows, -1)


def solution(mesh):
    in_specs = (
        P(ROWS, "tp"),
        P(ROWS, "tp"),
        P(ROWS, "tp"),
        P(ROWS, None, "tp"),
        P(ROWS, None, "tp"),
        P(),
        P(),
        P(ROWS, "tp"),
    )
    out_specs = P(ROWS, None)
    rows, parts = mesh.devices.shape
    cores = 2
    depth = 4 if rows % (4 * cores) == 0 else 1
    split = Mesh(mesh.devices.reshape(depth, rows // (depth * cores), cores, parts), ROWS + ("tp",))
    return jax.shard_map(shards, mesh=split, in_specs=in_specs, out_specs=out_specs, check_vma=False)
```

```python
import math

import jax
import jax.numpy as jnp
from jax import lax
from jax.sharding import Mesh
from jax.sharding import PartitionSpec as P

HD = 128
GROUP = 5
ROWS = ("z", "x", "core")


ROPE_BASE = 1000000.0
FLOOR_SCORE = -1e30


def from_partner(value, axis, distance):
    return lax.ppermute(value, axis, [(i, i ^ 1 << distance) for i in range(lax.axis_size(axis))])


def rotate(values, places):
    inverse = 1.0 / ROPE_BASE ** (jnp.arange(0, HD, 2).astype(jnp.float32) / HD)
    angles = places.astype(jnp.float32)[:, None] * inverse[None, :]
    cosine = jnp.concatenate([jnp.cos(angles), jnp.cos(angles)], axis=-1)[:, None, :]
    sine = jnp.concatenate([jnp.sin(angles), jnp.sin(angles)], axis=-1)[:, None, :]
    first_half = values[..., : HD // 2]
    second_half = values[..., HD // 2 :]
    turned = jnp.concatenate([-second_half, first_half], axis=-1)
    return values * cosine + turned * sine


def absorb(state, queries, block_keys, block_values, allowed, scale):
    running_max, running_sum, output = state
    scores = (
        jnp.einsum("qcgd,kcd->cgqk", queries, block_keys, preferred_element_type=jnp.float32)
        * scale
    )
    scores = jnp.where(allowed[None, None], scores, FLOOR_SCORE)
    new_max = jnp.maximum(running_max, jnp.max(scores, axis=-1))
    factor = jnp.exp(running_max - new_max)
    weights = jnp.where(allowed[None, None], jnp.exp(scores - new_max[..., None]), 0.0)
    running_sum = running_sum * factor + jnp.sum(weights, axis=-1)
    mixed = jnp.einsum(
        "cgqk,kcd->qcgd",
        weights.astype(jnp.bfloat16),
        block_values,
        preferred_element_type=jnp.float32,
    )
    output = output * jnp.transpose(factor, (2, 0, 1))[..., None] + mixed
    return (new_max, running_sum, output)


def output_rows(w_out):
    parts = lax.axis_size("tp")
    rows, width = w_out.shape
    share = rows // parts
    pieces = lax.all_to_all(w_out.reshape(parts, share, width), "tp", 0, 0, tiled=True)
    mine = jnp.transpose(pieces, (1, 0, 2))
    near = lax.all_gather(mine, "z", axis=0, tiled=True)
    return lax.all_gather(near, ("x", "core"), axis=0, tiled=True), share


def shards(q_new, k_new, v_new, k_cache, v_cache, lengths, page_table, w_out):
    own_rows = q_new.shape[0]
    all_rows = 2 * own_rows
    local_heads = k_new.shape[1] // HD
    pages_local = k_cache.shape[0]
    page_rows = k_cache.shape[1]
    scale = 1.0 / math.sqrt(HD)
    weights_mine, share = output_rows(w_out)
    device_row = (lax.axis_index("z") * lax.axis_size("x") + lax.axis_index("x")) * lax.axis_size(
        "core"
    ) + lax.axis_index("core")
    parity = device_row % 2
    request = device_row // 2
    length = lengths[request]
    own_places = length + parity * own_rows + jnp.arange(own_rows)
    own_queries = rotate(
        q_new.reshape(own_rows, local_heads * GROUP, HD).astype(jnp.float32), own_places
    ).astype(jnp.bfloat16)
    own_keys = rotate(
        k_new.reshape(own_rows, local_heads, HD).astype(jnp.float32), own_places
    ).astype(jnp.bfloat16)
    own_values = v_new.reshape(own_rows, local_heads, HD)
    query_heads = own_queries.shape[1]
    peer_pack = from_partner(
        jnp.concatenate([own_queries, own_keys, own_values], axis=1), "core", 0
    )
    peer_queries = peer_pack[:, :query_heads]
    peer_keys = peer_pack[:, query_heads : query_heads + local_heads]
    peer_values = peer_pack[:, query_heads + local_heads :]

    def ordered(mine, theirs):
        return jnp.where(
            parity == 0,
            jnp.concatenate([mine, theirs], axis=0),
            jnp.concatenate([theirs, mine], axis=0),
        )

    queries = ordered(own_queries, peer_queries).reshape(all_rows, local_heads, GROUP, HD)
    fresh_keys = ordered(own_keys, peer_keys)
    fresh_values = ordered(own_values, peer_values)
    state = (
        jnp.full((local_heads, GROUP, all_rows), FLOOR_SCORE, jnp.float32),
        jnp.zeros((local_heads, GROUP, all_rows), jnp.float32),
        jnp.zeros((all_rows, local_heads, GROUP, HD), jnp.float32),
    )
    token_index = jnp.arange(all_rows)
    causal = (token_index[None, :] <= token_index[:, None]) & (parity == 1)
    state = absorb(state, queries, fresh_keys, fresh_values, causal, scale)
    page_count = (length + page_rows - 1) // page_rows
    even_pages = (page_count + 1) // 2
    first_page = jnp.where(parity == 0, 0, even_pages)
    last_page = jnp.where(parity == 0, even_pages, page_count)
    table_row = page_table[request]
    logical = jnp.arange(table_row.shape[0])
    in_range = (logical >= first_page) & (logical < last_page)
    offset = device_row * pages_local
    slot_ids = jnp.arange(pages_local)
    match = in_range[:, None] & (table_row[:, None] - offset == slot_ids[None, :])
    used = jnp.any(match, axis=0)
    base = jnp.sum(jnp.where(match, logical[:, None], 0), axis=0) * page_rows
    key_places = (base[:, None] + jnp.arange(page_rows)[None, :]).reshape(-1)
    usable = jnp.repeat(used, page_rows) & (key_places < length)
    allowed = jnp.broadcast_to(usable[None, :], (all_rows, pages_local * page_rows))
    pool_keys = k_cache.reshape(pages_local * page_rows, local_heads, HD)
    pool_values = v_cache.reshape(pages_local * page_rows, local_heads, HD)
    running_max, running_sum, output = absorb(
        state, queries, pool_keys, pool_values, allowed, scale
    )
    peer_start = (1 - parity) * own_rows
    own_start = parity * own_rows
    outgoing = (
        lax.dynamic_slice_in_dim(output, peer_start, own_rows, 0),
        lax.dynamic_slice_in_dim(running_max, peer_start, own_rows, 2),
        lax.dynamic_slice_in_dim(running_sum, peer_start, own_rows, 2),
    )
    outgoing = jnp.concatenate(
        [
            outgoing[0].astype(jnp.bfloat16),
            jnp.transpose(outgoing[1], (2, 0, 1))[..., None].astype(jnp.bfloat16),
            jnp.transpose(outgoing[2], (2, 0, 1))[..., None].astype(jnp.bfloat16),
        ],
        axis=-1,
    )
    incoming = from_partner(outgoing, "core", 0).astype(jnp.float32)
    other_output = incoming[..., :HD]
    other_max = jnp.transpose(incoming[..., HD], (1, 2, 0))
    other_sum = jnp.transpose(incoming[..., HD + 1], (1, 2, 0))
    mine_output = lax.dynamic_slice_in_dim(output, own_start, own_rows, 0)
    mine_max = lax.dynamic_slice_in_dim(running_max, own_start, own_rows, 2)
    mine_sum = lax.dynamic_slice_in_dim(running_sum, own_start, own_rows, 2)
    joint_max = jnp.maximum(mine_max, other_max)
    mine_factor = jnp.exp(mine_max - joint_max)
    other_factor = jnp.exp(other_max - joint_max)
    joint_sum = mine_sum * mine_factor + other_sum * other_factor
    joint_output = (
        mine_output * jnp.transpose(mine_factor, (2, 0, 1))[..., None]
        + other_output * jnp.transpose(other_factor, (2, 0, 1))[..., None]
    )
    attention = (
        (joint_output / jnp.transpose(joint_sum, (2, 0, 1))[..., None])
        .reshape(own_rows, local_heads * GROUP * HD)
        .astype(jnp.bfloat16)
    )
    full_rows = lax.all_gather(attention[:, None], "tp", axis=1, tiled=True)
    projected = lax.dot_general(
        full_rows,
        weights_mine,
        (((1, 2), (1, 2)), ((), ())),
        preferred_element_type=jnp.float32,
    )
    depth = lax.axis_size("z")
    projected = projected.reshape(own_rows, -1, depth, share)
    projected = jnp.transpose(projected, (0, 2, 1, 3)).reshape(own_rows, -1, share)
    projected = projected.astype(jnp.bfloat16)
    gathered = lax.all_gather(projected, "tp", axis=2, tiled=True)
    return gathered.reshape(own_rows, -1)


def solution(mesh):
    in_specs = (
        P(ROWS, "tp"),
        P(ROWS, "tp"),
        P(ROWS, "tp"),
        P(ROWS, None, "tp"),
        P(ROWS, None, "tp"),
        P(),
        P(),
        P(ROWS, "tp"),
    )
    out_specs = P(ROWS, None)
    rows, parts = mesh.devices.shape
    cores = 2
    depth = 4 if rows % (4 * cores) == 0 else 1
    split = Mesh(mesh.devices.reshape(depth, rows // (depth * cores), cores, parts), ROWS + ("tp",))
    return jax.shard_map(shards, mesh=split, in_specs=in_specs, out_specs=out_specs, check_vma=False)
```

```python
import math

import jax
import jax.numpy as jnp
from jax import lax
from jax.sharding import Mesh
from jax.sharding import PartitionSpec as P

HD = 128
GROUP = 5
ROWS = ("z", "x", "core")


ROPE_BASE = 1000000.0
FLOOR_SCORE = -1e30


def from_partner(value, axis, distance):
    return lax.ppermute(value, axis, [(i, i ^ 1 << distance) for i in range(lax.axis_size(axis))])


def rotate(values, places):
    inverse = 1.0 / ROPE_BASE ** (jnp.arange(0, HD, 2).astype(jnp.float32) / HD)
    angles = places.astype(jnp.float32)[:, None] * inverse[None, :]
    cosine = jnp.concatenate([jnp.cos(angles), jnp.cos(angles)], axis=-1)[:, None, :]
    sine = jnp.concatenate([jnp.sin(angles), jnp.sin(angles)], axis=-1)[:, None, :]
    first_half = values[..., : HD // 2]
    second_half = values[..., HD // 2 :]
    turned = jnp.concatenate([-second_half, first_half], axis=-1)
    return values * cosine + turned * sine


def absorb(state, queries, block_keys, block_values, allowed, scale):
    running_max, running_sum, output = state
    scores = (
        jnp.einsum("qcgd,kcd->cgqk", queries, block_keys, preferred_element_type=jnp.float32)
        * scale
    )
    scores = jnp.where(allowed[None, None], scores, FLOOR_SCORE)
    new_max = jnp.maximum(running_max, jnp.max(scores, axis=-1))
    factor = jnp.exp(running_max - new_max)
    weights = jnp.where(allowed[None, None], jnp.exp(scores - new_max[..., None]), 0.0)
    running_sum = running_sum * factor + jnp.sum(weights, axis=-1)
    mixed = jnp.einsum(
        "cgqk,kcd->qcgd",
        weights.astype(jnp.bfloat16),
        block_values,
        preferred_element_type=jnp.float32,
    )
    output = output * jnp.transpose(factor, (2, 0, 1))[..., None] + mixed
    return (new_max, running_sum, output)


def output_rows(w_out):
    parts = lax.axis_size("tp")
    depth = lax.axis_size("z")
    rows, width = w_out.shape
    share = rows // parts
    chunks = jnp.broadcast_to(w_out.reshape(1, parts, share, width), (depth, parts, share, width))
    pieces = lax.all_to_all(
        chunks.reshape(depth * parts, share, width), ("z", "tp"), 0, 0, tiled=True
    )
    near = jnp.transpose(pieces.reshape(depth, parts, share, width), (0, 2, 1, 3))
    near = near.reshape(depth * share, parts, width)
    return lax.all_gather(near, ("x", "core"), axis=0, tiled=True), share


def shards(q_new, k_new, v_new, k_cache, v_cache, lengths, page_table, w_out):
    own_rows = q_new.shape[0]
    all_rows = 2 * own_rows
    local_heads = k_new.shape[1] // HD
    pages_local = k_cache.shape[0]
    page_rows = k_cache.shape[1]
    scale = 1.0 / math.sqrt(HD)
    weights_mine, share = output_rows(w_out)
    device_row = (lax.axis_index("z") * lax.axis_size("x") + lax.axis_index("x")) * lax.axis_size(
        "core"
    ) + lax.axis_index("core")
    parity = device_row % 2
    request = device_row // 2
    length = lengths[request]
    own_places = length + parity * own_rows + jnp.arange(own_rows)
    own_queries = rotate(
        q_new.reshape(own_rows, local_heads * GROUP, HD).astype(jnp.float32), own_places
    ).astype(jnp.bfloat16)
    own_keys = rotate(
        k_new.reshape(own_rows, local_heads, HD).astype(jnp.float32), own_places
    ).astype(jnp.bfloat16)
    own_values = v_new.reshape(own_rows, local_heads, HD)
    query_heads = own_queries.shape[1]
    peer_pack = from_partner(
        jnp.concatenate([own_queries, own_keys, own_values], axis=1), "core", 0
    )
    peer_queries = peer_pack[:, :query_heads]
    peer_keys = peer_pack[:, query_heads : query_heads + local_heads]
    peer_values = peer_pack[:, query_heads + local_heads :]

    def ordered(mine, theirs):
        return jnp.where(
            parity == 0,
            jnp.concatenate([mine, theirs], axis=0),
            jnp.concatenate([theirs, mine], axis=0),
        )

    queries = ordered(own_queries, peer_queries).reshape(all_rows, local_heads, GROUP, HD)
    fresh_keys = ordered(own_keys, peer_keys)
    fresh_values = ordered(own_values, peer_values)
    state = (
        jnp.full((local_heads, GROUP, all_rows), FLOOR_SCORE, jnp.float32),
        jnp.zeros((local_heads, GROUP, all_rows), jnp.float32),
        jnp.zeros((all_rows, local_heads, GROUP, HD), jnp.float32),
    )
    token_index = jnp.arange(all_rows)
    causal = (token_index[None, :] <= token_index[:, None]) & (parity == 1)
    state = absorb(state, queries, fresh_keys, fresh_values, causal, scale)
    page_count = (length + page_rows - 1) // page_rows
    even_pages = (page_count + 1) // 2
    first_page = jnp.where(parity == 0, 0, even_pages)
    last_page = jnp.where(parity == 0, even_pages, page_count)
    table_row = page_table[request]
    logical = jnp.arange(table_row.shape[0])
    in_range = (logical >= first_page) & (logical < last_page)
    offset = device_row * pages_local
    slot_ids = jnp.arange(pages_local)
    match = in_range[:, None] & (table_row[:, None] - offset == slot_ids[None, :])
    used = jnp.any(match, axis=0)
    base = jnp.sum(jnp.where(match, logical[:, None], 0), axis=0) * page_rows
    key_places = (base[:, None] + jnp.arange(page_rows)[None, :]).reshape(-1)
    usable = jnp.repeat(used, page_rows) & (key_places < length)
    allowed = jnp.broadcast_to(usable[None, :], (all_rows, pages_local * page_rows))
    pool_keys = k_cache.reshape(pages_local * page_rows, local_heads, HD)
    pool_values = v_cache.reshape(pages_local * page_rows, local_heads, HD)
    running_max, running_sum, output = absorb(
        state, queries, pool_keys, pool_values, allowed, scale
    )
    peer_start = (1 - parity) * own_rows
    own_start = parity * own_rows
    outgoing = (
        lax.dynamic_slice_in_dim(output, peer_start, own_rows, 0),
        lax.dynamic_slice_in_dim(running_max, peer_start, own_rows, 2),
        lax.dynamic_slice_in_dim(running_sum, peer_start, own_rows, 2),
    )
    outgoing = jnp.concatenate(
        [
            outgoing[0].astype(jnp.bfloat16),
            jnp.transpose(outgoing[1], (2, 0, 1))[..., None].astype(jnp.bfloat16),
            jnp.transpose(outgoing[2], (2, 0, 1))[..., None].astype(jnp.bfloat16),
        ],
        axis=-1,
    )
    incoming = from_partner(outgoing, "core", 0).astype(jnp.float32)
    other_output = incoming[..., :HD]
    other_max = jnp.transpose(incoming[..., HD], (1, 2, 0))
    other_sum = jnp.transpose(incoming[..., HD + 1], (1, 2, 0))
    mine_output = lax.dynamic_slice_in_dim(output, own_start, own_rows, 0)
    mine_max = lax.dynamic_slice_in_dim(running_max, own_start, own_rows, 2)
    mine_sum = lax.dynamic_slice_in_dim(running_sum, own_start, own_rows, 2)
    joint_max = jnp.maximum(mine_max, other_max)
    mine_factor = jnp.exp(mine_max - joint_max)
    other_factor = jnp.exp(other_max - joint_max)
    joint_sum = mine_sum * mine_factor + other_sum * other_factor
    joint_output = (
        mine_output * jnp.transpose(mine_factor, (2, 0, 1))[..., None]
        + other_output * jnp.transpose(other_factor, (2, 0, 1))[..., None]
    )
    attention = (
        (joint_output / jnp.transpose(joint_sum, (2, 0, 1))[..., None])
        .reshape(own_rows, local_heads * GROUP * HD)
        .astype(jnp.bfloat16)
    )
    full_rows = lax.all_gather(attention[:, None], "tp", axis=1, tiled=True)
    projected = lax.dot_general(
        full_rows,
        weights_mine,
        (((1, 2), (1, 2)), ((), ())),
        preferred_element_type=jnp.float32,
    )
    depth = lax.axis_size("z")
    projected = projected.reshape(own_rows, -1, depth, share)
    projected = jnp.transpose(projected, (0, 2, 1, 3)).reshape(own_rows, -1, share)
    projected = projected.astype(jnp.bfloat16)
    gathered = lax.all_gather(projected, "tp", axis=2, tiled=True)
    return gathered.reshape(own_rows, -1)


def solution(mesh):
    in_specs = (
        P(ROWS, "tp"),
        P(ROWS, "tp"),
        P(ROWS, "tp"),
        P(ROWS, None, "tp"),
        P(ROWS, None, "tp"),
        P(),
        P(),
        P(ROWS, "tp"),
    )
    out_specs = P(ROWS, None)
    rows, parts = mesh.devices.shape
    cores = 2
    depth = 4 if rows % (4 * cores) == 0 else 1
    split = Mesh(mesh.devices.reshape(depth, rows // (depth * cores), cores, parts), ROWS + ("tp",))
    return jax.shard_map(shards, mesh=split, in_specs=in_specs, out_specs=out_specs, check_vma=False)
```

```python
import math

import jax
import jax.numpy as jnp
from jax import lax
from jax.sharding import Mesh
from jax.sharding import PartitionSpec as P

HD = 128
GROUP = 5
ROWS = ("z", "x", "core")


ROPE_BASE = 1000000.0
FLOOR_SCORE = -1e30


def from_partner(value, axis, distance):
    return lax.ppermute(value, axis, [(i, i ^ 1 << distance) for i in range(lax.axis_size(axis))])


def rotate(values, places):
    inverse = 1.0 / ROPE_BASE ** (jnp.arange(0, HD, 2).astype(jnp.float32) / HD)
    angles = places.astype(jnp.float32)[:, None] * inverse[None, :]
    cosine = jnp.concatenate([jnp.cos(angles), jnp.cos(angles)], axis=-1)[:, None, :]
    sine = jnp.concatenate([jnp.sin(angles), jnp.sin(angles)], axis=-1)[:, None, :]
    first_half = values[..., : HD // 2]
    second_half = values[..., HD // 2 :]
    turned = jnp.concatenate([-second_half, first_half], axis=-1)
    return values * cosine + turned * sine


def absorb(state, queries, block_keys, block_values, allowed, scale):
    running_max, running_sum, output = state
    scores = (
        jnp.einsum("qcgd,kcd->cgqk", queries, block_keys, preferred_element_type=jnp.float32)
        * scale
    )
    scores = jnp.where(allowed[None, None], scores, FLOOR_SCORE)
    new_max = jnp.maximum(running_max, jnp.max(scores, axis=-1))
    factor = jnp.exp(running_max - new_max)
    weights = jnp.where(allowed[None, None], jnp.exp(scores - new_max[..., None]), 0.0)
    running_sum = running_sum * factor + jnp.sum(weights, axis=-1)
    mixed = jnp.einsum(
        "cgqk,kcd->qcgd",
        weights.astype(jnp.bfloat16),
        block_values,
        preferred_element_type=jnp.float32,
    )
    output = output * jnp.transpose(factor, (2, 0, 1))[..., None] + mixed
    return (new_max, running_sum, output)


def output_rows(w_out):
    parts = lax.axis_size("tp")
    rows, width = w_out.shape
    share = rows // parts
    pieces = lax.all_to_all(w_out.reshape(parts, share, width), "tp", 0, 0, tiled=True)
    near = jnp.transpose(pieces, (1, 0, 2))
    depth = lax.axis_size("z")
    place = lax.axis_index("z")
    step = 1
    while step < depth:
        other = lax.ppermute(near, "z", [(i, i ^ step) for i in range(depth)])
        near = jnp.where(
            (place & step) == 0,
            jnp.concatenate([near, other], axis=0),
            jnp.concatenate([other, near], axis=0),
        )
        step *= 2
    return lax.all_gather(near, ("x", "core"), axis=0, tiled=True), share


def shards(q_new, k_new, v_new, k_cache, v_cache, lengths, page_table, w_out):
    own_rows = q_new.shape[0]
    all_rows = 2 * own_rows
    local_heads = k_new.shape[1] // HD
    pages_local = k_cache.shape[0]
    page_rows = k_cache.shape[1]
    scale = 1.0 / math.sqrt(HD)
    weights_mine, share = output_rows(w_out)
    device_row = (lax.axis_index("z") * lax.axis_size("x") + lax.axis_index("x")) * lax.axis_size(
        "core"
    ) + lax.axis_index("core")
    parity = device_row % 2
    request = device_row // 2
    length = lengths[request]
    own_places = length + parity * own_rows + jnp.arange(own_rows)
    own_queries = rotate(
        q_new.reshape(own_rows, local_heads * GROUP, HD).astype(jnp.float32), own_places
    ).astype(jnp.bfloat16)
    own_keys = rotate(
        k_new.reshape(own_rows, local_heads, HD).astype(jnp.float32), own_places
    ).astype(jnp.bfloat16)
    own_values = v_new.reshape(own_rows, local_heads, HD)
    query_heads = own_queries.shape[1]
    peer_pack = from_partner(
        jnp.concatenate([own_queries, own_keys, own_values], axis=1), "core", 0
    )
    peer_queries = peer_pack[:, :query_heads]
    peer_keys = peer_pack[:, query_heads : query_heads + local_heads]
    peer_values = peer_pack[:, query_heads + local_heads :]

    def ordered(mine, theirs):
        return jnp.where(
            parity == 0,
            jnp.concatenate([mine, theirs], axis=0),
            jnp.concatenate([theirs, mine], axis=0),
        )

    queries = ordered(own_queries, peer_queries).reshape(all_rows, local_heads, GROUP, HD)
    fresh_keys = ordered(own_keys, peer_keys)
    fresh_values = ordered(own_values, peer_values)
    state = (
        jnp.full((local_heads, GROUP, all_rows), FLOOR_SCORE, jnp.float32),
        jnp.zeros((local_heads, GROUP, all_rows), jnp.float32),
        jnp.zeros((all_rows, local_heads, GROUP, HD), jnp.float32),
    )
    token_index = jnp.arange(all_rows)
    causal = (token_index[None, :] <= token_index[:, None]) & (parity == 1)
    state = absorb(state, queries, fresh_keys, fresh_values, causal, scale)
    page_count = (length + page_rows - 1) // page_rows
    even_pages = (page_count + 1) // 2
    first_page = jnp.where(parity == 0, 0, even_pages)
    last_page = jnp.where(parity == 0, even_pages, page_count)
    table_row = page_table[request]
    logical = jnp.arange(table_row.shape[0])
    in_range = (logical >= first_page) & (logical < last_page)
    offset = device_row * pages_local
    slot_ids = jnp.arange(pages_local)
    match = in_range[:, None] & (table_row[:, None] - offset == slot_ids[None, :])
    used = jnp.any(match, axis=0)
    base = jnp.sum(jnp.where(match, logical[:, None], 0), axis=0) * page_rows
    key_places = (base[:, None] + jnp.arange(page_rows)[None, :]).reshape(-1)
    usable = jnp.repeat(used, page_rows) & (key_places < length)
    allowed = jnp.broadcast_to(usable[None, :], (all_rows, pages_local * page_rows))
    pool_keys = k_cache.reshape(pages_local * page_rows, local_heads, HD)
    pool_values = v_cache.reshape(pages_local * page_rows, local_heads, HD)
    running_max, running_sum, output = absorb(
        state, queries, pool_keys, pool_values, allowed, scale
    )
    peer_start = (1 - parity) * own_rows
    own_start = parity * own_rows
    outgoing = (
        lax.dynamic_slice_in_dim(output, peer_start, own_rows, 0),
        lax.dynamic_slice_in_dim(running_max, peer_start, own_rows, 2),
        lax.dynamic_slice_in_dim(running_sum, peer_start, own_rows, 2),
    )
    outgoing = jnp.concatenate(
        [
            outgoing[0].astype(jnp.bfloat16),
            jnp.transpose(outgoing[1], (2, 0, 1))[..., None].astype(jnp.bfloat16),
            jnp.transpose(outgoing[2], (2, 0, 1))[..., None].astype(jnp.bfloat16),
        ],
        axis=-1,
    )
    incoming = from_partner(outgoing, "core", 0).astype(jnp.float32)
    other_output = incoming[..., :HD]
    other_max = jnp.transpose(incoming[..., HD], (1, 2, 0))
    other_sum = jnp.transpose(incoming[..., HD + 1], (1, 2, 0))
    mine_output = lax.dynamic_slice_in_dim(output, own_start, own_rows, 0)
    mine_max = lax.dynamic_slice_in_dim(running_max, own_start, own_rows, 2)
    mine_sum = lax.dynamic_slice_in_dim(running_sum, own_start, own_rows, 2)
    joint_max = jnp.maximum(mine_max, other_max)
    mine_factor = jnp.exp(mine_max - joint_max)
    other_factor = jnp.exp(other_max - joint_max)
    joint_sum = mine_sum * mine_factor + other_sum * other_factor
    joint_output = (
        mine_output * jnp.transpose(mine_factor, (2, 0, 1))[..., None]
        + other_output * jnp.transpose(other_factor, (2, 0, 1))[..., None]
    )
    attention = (
        (joint_output / jnp.transpose(joint_sum, (2, 0, 1))[..., None])
        .reshape(own_rows, local_heads * GROUP * HD)
        .astype(jnp.bfloat16)
    )
    full_rows = lax.all_gather(attention[:, None], "tp", axis=1, tiled=True)
    projected = lax.dot_general(
        full_rows,
        weights_mine,
        (((1, 2), (1, 2)), ((), ())),
        preferred_element_type=jnp.float32,
    )
    depth = lax.axis_size("z")
    projected = projected.reshape(own_rows, -1, depth, share)
    projected = jnp.transpose(projected, (0, 2, 1, 3)).reshape(own_rows, -1, share)
    projected = projected.astype(jnp.bfloat16)
    gathered = lax.all_gather(projected, "tp", axis=2, tiled=True)
    return gathered.reshape(own_rows, -1)


def solution(mesh):
    in_specs = (
        P(ROWS, "tp"),
        P(ROWS, "tp"),
        P(ROWS, "tp"),
        P(ROWS, None, "tp"),
        P(ROWS, None, "tp"),
        P(),
        P(),
        P(ROWS, "tp"),
    )
    out_specs = P(ROWS, None)
    rows, parts = mesh.devices.shape
    cores = 2
    depth = 4 if rows % (4 * cores) == 0 else 1
    split = Mesh(mesh.devices.reshape(depth, rows // (depth * cores), cores, parts), ROWS + ("tp",))
    return jax.shard_map(shards, mesh=split, in_specs=in_specs, out_specs=out_specs, check_vma=False)
```

```python
import math

import jax
import jax.numpy as jnp
from jax import lax
from jax.sharding import Mesh
from jax.sharding import PartitionSpec as P

HD = 128
GROUP = 5
ROWS = ("z", "x", "core")


ROPE_BASE = 1000000.0
FLOOR_SCORE = -1e30


def from_partner(value, axis, distance):
    return lax.ppermute(value, axis, [(i, i ^ 1 << distance) for i in range(lax.axis_size(axis))])


def rotate(values, places):
    inverse = 1.0 / ROPE_BASE ** (jnp.arange(0, HD, 2).astype(jnp.float32) / HD)
    angles = places.astype(jnp.float32)[:, None] * inverse[None, :]
    cosine = jnp.concatenate([jnp.cos(angles), jnp.cos(angles)], axis=-1)[:, None, :]
    sine = jnp.concatenate([jnp.sin(angles), jnp.sin(angles)], axis=-1)[:, None, :]
    first_half = values[..., : HD // 2]
    second_half = values[..., HD // 2 :]
    turned = jnp.concatenate([-second_half, first_half], axis=-1)
    return values * cosine + turned * sine


def absorb(state, queries, block_keys, block_values, allowed, scale):
    running_max, running_sum, output = state
    scores = (
        jnp.einsum("qcgd,kcd->cgqk", queries, block_keys, preferred_element_type=jnp.float32)
        * scale
    )
    scores = jnp.where(allowed[None, None], scores, FLOOR_SCORE)
    new_max = jnp.maximum(running_max, jnp.max(scores, axis=-1))
    factor = jnp.exp(running_max - new_max)
    weights = jnp.where(allowed[None, None], jnp.exp(scores - new_max[..., None]), 0.0)
    running_sum = running_sum * factor + jnp.sum(weights, axis=-1)
    mixed = jnp.einsum(
        "cgqk,kcd->qcgd",
        weights.astype(jnp.bfloat16),
        block_values,
        preferred_element_type=jnp.float32,
    )
    output = output * jnp.transpose(factor, (2, 0, 1))[..., None] + mixed
    return (new_max, running_sum, output)


def output_rows(w_out):
    parts = lax.axis_size("tp")
    depth = lax.axis_size("z")
    rows, width = w_out.shape
    share = rows // parts
    chunks = jnp.broadcast_to(w_out.reshape(1, parts, share, width), (depth, parts, share, width))
    pieces = lax.all_to_all(
        chunks.reshape(depth * parts, share, width), ("z", "tp"), 0, 0, tiled=True
    )
    near = jnp.transpose(pieces.reshape(depth, parts, share, width), (0, 2, 1, 3))
    near = near.reshape(depth * share, parts, width)
    return lax.all_gather(near, ("x", "core"), axis=0, tiled=True), share


def shards(q_new, k_new, v_new, k_cache, v_cache, lengths, page_table, w_out):
    own_rows = q_new.shape[0]
    all_rows = 2 * own_rows
    local_heads = k_new.shape[1] // HD
    pages_local = k_cache.shape[0]
    page_rows = k_cache.shape[1]
    scale = 1.0 / math.sqrt(HD)
    weights_mine, share = output_rows(w_out)
    device_row = (lax.axis_index("z") * lax.axis_size("x") + lax.axis_index("x")) * lax.axis_size(
        "core"
    ) + lax.axis_index("core")
    parity = device_row % 2
    request = device_row // 2
    length = lengths[request]
    own_places = length + parity * own_rows + jnp.arange(own_rows)
    own_queries = rotate(
        q_new.reshape(own_rows, local_heads * GROUP, HD).astype(jnp.float32), own_places
    ).astype(jnp.bfloat16)
    own_keys = rotate(
        k_new.reshape(own_rows, local_heads, HD).astype(jnp.float32), own_places
    ).astype(jnp.bfloat16)
    own_values = v_new.reshape(own_rows, local_heads, HD)
    query_heads = own_queries.shape[1]
    peer_pack = from_partner(
        jnp.concatenate([own_queries, own_keys, own_values], axis=1), "core", 0
    )
    peer_queries = peer_pack[:, :query_heads]
    peer_keys = peer_pack[:, query_heads : query_heads + local_heads]
    peer_values = peer_pack[:, query_heads + local_heads :]

    def ordered(mine, theirs):
        return jnp.where(
            parity == 0,
            jnp.concatenate([mine, theirs], axis=0),
            jnp.concatenate([theirs, mine], axis=0),
        )

    queries = ordered(own_queries, peer_queries).reshape(all_rows, local_heads, GROUP, HD)
    fresh_keys = ordered(own_keys, peer_keys)
    fresh_values = ordered(own_values, peer_values)
    state = (
        jnp.full((local_heads, GROUP, all_rows), FLOOR_SCORE, jnp.float32),
        jnp.zeros((local_heads, GROUP, all_rows), jnp.float32),
        jnp.zeros((all_rows, local_heads, GROUP, HD), jnp.float32),
    )
    token_index = jnp.arange(all_rows)
    causal = (token_index[None, :] <= token_index[:, None]) & (parity == 1)
    state = absorb(state, queries, fresh_keys, fresh_values, causal, scale)
    page_count = (length + page_rows - 1) // page_rows
    even_pages = (page_count + 1) // 2
    first_page = jnp.where(parity == 0, 0, even_pages)
    last_page = jnp.where(parity == 0, even_pages, page_count)
    table_row = page_table[request]
    logical = jnp.arange(table_row.shape[0])
    in_range = (logical >= first_page) & (logical < last_page)
    offset = device_row * pages_local
    slot_ids = jnp.arange(pages_local)
    match = in_range[:, None] & (table_row[:, None] - offset == slot_ids[None, :])
    used = jnp.any(match, axis=0)
    base = jnp.sum(jnp.where(match, logical[:, None], 0), axis=0) * page_rows
    key_places = (base[:, None] + jnp.arange(page_rows)[None, :]).reshape(-1)
    usable = jnp.repeat(used, page_rows) & (key_places < length)
    allowed = jnp.broadcast_to(usable[None, :], (all_rows, pages_local * page_rows))
    pool_keys = k_cache.reshape(pages_local * page_rows, local_heads, HD)
    pool_values = v_cache.reshape(pages_local * page_rows, local_heads, HD)
    half = pool_keys.shape[0] // 2
    for start in (0, half):
        state = absorb(
            state,
            queries,
            pool_keys[start : start + half],
            pool_values[start : start + half],
            allowed[:, start : start + half],
            scale,
        )
    running_max, running_sum, output = state
    peer_start = (1 - parity) * own_rows
    own_start = parity * own_rows
    outgoing = (
        lax.dynamic_slice_in_dim(output, peer_start, own_rows, 0),
        lax.dynamic_slice_in_dim(running_max, peer_start, own_rows, 2),
        lax.dynamic_slice_in_dim(running_sum, peer_start, own_rows, 2),
    )
    outgoing = jnp.concatenate(
        [
            outgoing[0].astype(jnp.bfloat16),
            jnp.transpose(outgoing[1], (2, 0, 1))[..., None].astype(jnp.bfloat16),
            jnp.transpose(outgoing[2], (2, 0, 1))[..., None].astype(jnp.bfloat16),
        ],
        axis=-1,
    )
    incoming = from_partner(outgoing, "core", 0).astype(jnp.float32)
    other_output = incoming[..., :HD]
    other_max = jnp.transpose(incoming[..., HD], (1, 2, 0))
    other_sum = jnp.transpose(incoming[..., HD + 1], (1, 2, 0))
    mine_output = lax.dynamic_slice_in_dim(output, own_start, own_rows, 0)
    mine_max = lax.dynamic_slice_in_dim(running_max, own_start, own_rows, 2)
    mine_sum = lax.dynamic_slice_in_dim(running_sum, own_start, own_rows, 2)
    joint_max = jnp.maximum(mine_max, other_max)
    mine_factor = jnp.exp(mine_max - joint_max)
    other_factor = jnp.exp(other_max - joint_max)
    joint_sum = mine_sum * mine_factor + other_sum * other_factor
    joint_output = (
        mine_output * jnp.transpose(mine_factor, (2, 0, 1))[..., None]
        + other_output * jnp.transpose(other_factor, (2, 0, 1))[..., None]
    )
    attention = (
        (joint_output / jnp.transpose(joint_sum, (2, 0, 1))[..., None])
        .reshape(own_rows, local_heads * GROUP * HD)
        .astype(jnp.bfloat16)
    )
    full_rows = lax.all_gather(attention[:, None], "tp", axis=1, tiled=True)
    projected = lax.dot_general(
        full_rows,
        weights_mine,
        (((1, 2), (1, 2)), ((), ())),
        preferred_element_type=jnp.float32,
    )
    depth = lax.axis_size("z")
    projected = projected.reshape(own_rows, -1, depth, share)
    projected = jnp.transpose(projected, (0, 2, 1, 3)).reshape(own_rows, -1, share)
    projected = projected.astype(jnp.bfloat16)
    gathered = lax.all_gather(projected, "tp", axis=2, tiled=True)
    return gathered.reshape(own_rows, -1)


def solution(mesh):
    in_specs = (
        P(ROWS, "tp"),
        P(ROWS, "tp"),
        P(ROWS, "tp"),
        P(ROWS, None, "tp"),
        P(ROWS, None, "tp"),
        P(),
        P(),
        P(ROWS, "tp"),
    )
    out_specs = P(ROWS, None)
    rows, parts = mesh.devices.shape
    cores = 2
    depth = 4 if rows % (4 * cores) == 0 else 1
    split = Mesh(mesh.devices.reshape(depth, rows // (depth * cores), cores, parts), ROWS + ("tp",))
    return jax.shard_map(shards, mesh=split, in_specs=in_specs, out_specs=out_specs, check_vma=False)
```

```python
import math

import jax
import jax.numpy as jnp
from jax import lax
from jax.sharding import Mesh
from jax.sharding import PartitionSpec as P

HD = 128
GROUP = 5
ROWS = ("z", "x", "core")


ROPE_BASE = 1000000.0
FLOOR_SCORE = -1e30


def from_partner(value, axis, distance):
    return lax.ppermute(value, axis, [(i, i ^ 1 << distance) for i in range(lax.axis_size(axis))])


def rotate(values, places):
    inverse = 1.0 / ROPE_BASE ** (jnp.arange(0, HD, 2).astype(jnp.float32) / HD)
    angles = places.astype(jnp.float32)[:, None] * inverse[None, :]
    cosine = jnp.concatenate([jnp.cos(angles), jnp.cos(angles)], axis=-1)[:, None, :]
    sine = jnp.concatenate([jnp.sin(angles), jnp.sin(angles)], axis=-1)[:, None, :]
    first_half = values[..., : HD // 2]
    second_half = values[..., HD // 2 :]
    turned = jnp.concatenate([-second_half, first_half], axis=-1)
    return values * cosine + turned * sine


def absorb(state, queries, block_keys, block_values, allowed, scale):
    running_max, running_sum, output = state
    scores = (
        jnp.einsum("qcgd,kcd->cgqk", queries, block_keys, preferred_element_type=jnp.float32)
        * scale
    )
    scores = jnp.where(allowed[None, None], scores, FLOOR_SCORE)
    new_max = jnp.maximum(running_max, jnp.max(scores, axis=-1))
    factor = jnp.exp(running_max - new_max)
    weights = jnp.where(allowed[None, None], jnp.exp(scores - new_max[..., None]), 0.0)
    running_sum = running_sum * factor + jnp.sum(weights, axis=-1)
    mixed = jnp.einsum(
        "cgqk,kcd->qcgd",
        weights.astype(jnp.bfloat16),
        block_values,
        preferred_element_type=jnp.float32,
    )
    output = output * jnp.transpose(factor, (2, 0, 1))[..., None] + mixed
    return (new_max, running_sum, output)


def output_rows(w_out):
    parts = lax.axis_size("tp")
    depth = lax.axis_size("z")
    rows, width = w_out.shape
    share = rows // parts
    chunks = jnp.broadcast_to(w_out.reshape(1, parts, share, width), (depth, parts, share, width))
    pieces = lax.all_to_all(
        chunks.reshape(depth * parts, share, width), ("z", "tp"), 0, 0, tiled=True
    )
    near = jnp.transpose(pieces.reshape(depth, parts, share, width), (0, 2, 1, 3))
    near = near.reshape(depth * share, parts, width)
    return lax.all_gather(near, ("x", "core"), axis=0, tiled=True), share


def shards(q_new, k_new, v_new, k_cache, v_cache, lengths, page_table, w_out):
    own_rows = q_new.shape[0]
    all_rows = 2 * own_rows
    local_heads = k_new.shape[1] // HD
    pages_local = k_cache.shape[0]
    page_rows = k_cache.shape[1]
    scale = 1.0 / math.sqrt(HD)
    weights_mine, share = output_rows(w_out)
    device_row = (lax.axis_index("z") * lax.axis_size("x") + lax.axis_index("x")) * lax.axis_size(
        "core"
    ) + lax.axis_index("core")
    parity = device_row % 2
    request = device_row // 2
    length = lengths[request]
    own_places = length + parity * own_rows + jnp.arange(own_rows)
    own_queries = rotate(
        q_new.reshape(own_rows, local_heads * GROUP, HD).astype(jnp.float32), own_places
    ).astype(jnp.bfloat16)
    own_keys = rotate(
        k_new.reshape(own_rows, local_heads, HD).astype(jnp.float32), own_places
    ).astype(jnp.bfloat16)
    own_values = v_new.reshape(own_rows, local_heads, HD)
    query_heads = own_queries.shape[1]
    peer_pack = from_partner(
        jnp.concatenate([own_queries, own_keys, own_values], axis=1), "core", 0
    )
    peer_queries = peer_pack[:, :query_heads]
    peer_keys = peer_pack[:, query_heads : query_heads + local_heads]
    peer_values = peer_pack[:, query_heads + local_heads :]

    def ordered(mine, theirs):
        return jnp.where(
            parity == 0,
            jnp.concatenate([mine, theirs], axis=0),
            jnp.concatenate([theirs, mine], axis=0),
        )

    queries = ordered(own_queries, peer_queries).reshape(all_rows, local_heads, GROUP, HD)
    fresh_keys = ordered(own_keys, peer_keys)
    fresh_values = ordered(own_values, peer_values)
    state = (
        jnp.full((local_heads, GROUP, all_rows), FLOOR_SCORE, jnp.float32),
        jnp.zeros((local_heads, GROUP, all_rows), jnp.float32),
        jnp.zeros((all_rows, local_heads, GROUP, HD), jnp.float32),
    )
    token_index = jnp.arange(all_rows)
    causal = (token_index[None, :] <= token_index[:, None]) & (parity == 1)
    state = absorb(state, queries, fresh_keys, fresh_values, causal, scale)
    page_count = (length + page_rows - 1) // page_rows
    even_pages = (page_count + 1) // 2
    first_page = jnp.where(parity == 0, 0, even_pages)
    last_page = jnp.where(parity == 0, even_pages, page_count)
    table_row = page_table[request]
    logical = jnp.arange(table_row.shape[0])
    in_range = (logical >= first_page) & (logical < last_page)
    offset = device_row * pages_local
    slot_ids = jnp.arange(pages_local)
    match = in_range[:, None] & (table_row[:, None] - offset == slot_ids[None, :])
    used = jnp.any(match, axis=0)
    base = jnp.sum(jnp.where(match, logical[:, None], 0), axis=0) * page_rows
    key_places = (base[:, None] + jnp.arange(page_rows)[None, :]).reshape(-1)
    usable = jnp.repeat(used, page_rows) & (key_places < length)
    allowed = jnp.broadcast_to(usable[None, :], (all_rows, pages_local * page_rows))
    pool_keys = k_cache.reshape(pages_local * page_rows, local_heads, HD)
    pool_values = v_cache.reshape(pages_local * page_rows, local_heads, HD)
    half = pool_keys.shape[0] // 4
    for start in range(0, pool_keys.shape[0], half):
        state = absorb(
            state,
            queries,
            pool_keys[start : start + half],
            pool_values[start : start + half],
            allowed[:, start : start + half],
            scale,
        )
    running_max, running_sum, output = state
    peer_start = (1 - parity) * own_rows
    own_start = parity * own_rows
    outgoing = (
        lax.dynamic_slice_in_dim(output, peer_start, own_rows, 0),
        lax.dynamic_slice_in_dim(running_max, peer_start, own_rows, 2),
        lax.dynamic_slice_in_dim(running_sum, peer_start, own_rows, 2),
    )
    outgoing = jnp.concatenate(
        [
            outgoing[0].astype(jnp.bfloat16),
            jnp.transpose(outgoing[1], (2, 0, 1))[..., None].astype(jnp.bfloat16),
            jnp.transpose(outgoing[2], (2, 0, 1))[..., None].astype(jnp.bfloat16),
        ],
        axis=-1,
    )
    incoming = from_partner(outgoing, "core", 0).astype(jnp.float32)
    other_output = incoming[..., :HD]
    other_max = jnp.transpose(incoming[..., HD], (1, 2, 0))
    other_sum = jnp.transpose(incoming[..., HD + 1], (1, 2, 0))
    mine_output = lax.dynamic_slice_in_dim(output, own_start, own_rows, 0)
    mine_max = lax.dynamic_slice_in_dim(running_max, own_start, own_rows, 2)
    mine_sum = lax.dynamic_slice_in_dim(running_sum, own_start, own_rows, 2)
    joint_max = jnp.maximum(mine_max, other_max)
    mine_factor = jnp.exp(mine_max - joint_max)
    other_factor = jnp.exp(other_max - joint_max)
    joint_sum = mine_sum * mine_factor + other_sum * other_factor
    joint_output = (
        mine_output * jnp.transpose(mine_factor, (2, 0, 1))[..., None]
        + other_output * jnp.transpose(other_factor, (2, 0, 1))[..., None]
    )
    attention = (
        (joint_output / jnp.transpose(joint_sum, (2, 0, 1))[..., None])
        .reshape(own_rows, local_heads * GROUP * HD)
        .astype(jnp.bfloat16)
    )
    full_rows = lax.all_gather(attention[:, None], "tp", axis=1, tiled=True)
    projected = lax.dot_general(
        full_rows,
        weights_mine,
        (((1, 2), (1, 2)), ((), ())),
        preferred_element_type=jnp.float32,
    )
    depth = lax.axis_size("z")
    projected = projected.reshape(own_rows, -1, depth, share)
    projected = jnp.transpose(projected, (0, 2, 1, 3)).reshape(own_rows, -1, share)
    projected = projected.astype(jnp.bfloat16)
    gathered = lax.all_gather(projected, "tp", axis=2, tiled=True)
    return gathered.reshape(own_rows, -1)


def solution(mesh):
    in_specs = (
        P(ROWS, "tp"),
        P(ROWS, "tp"),
        P(ROWS, "tp"),
        P(ROWS, None, "tp"),
        P(ROWS, None, "tp"),
        P(),
        P(),
        P(ROWS, "tp"),
    )
    out_specs = P(ROWS, None)
    rows, parts = mesh.devices.shape
    cores = 2
    depth = 4 if rows % (4 * cores) == 0 else 1
    split = Mesh(mesh.devices.reshape(depth, rows // (depth * cores), cores, parts), ROWS + ("tp",))
    return jax.shard_map(shards, mesh=split, in_specs=in_specs, out_specs=out_specs, check_vma=False)
```

```python
import math

import jax
import jax.numpy as jnp
from jax import lax
from jax.sharding import Mesh
from jax.sharding import PartitionSpec as P

HD = 128
GROUP = 5
ROWS = ("z", "x", "core")


ROPE_BASE = 1000000.0
FLOOR_SCORE = -1e30


def from_partner(value, axis, distance):
    return lax.ppermute(value, axis, [(i, i ^ 1 << distance) for i in range(lax.axis_size(axis))])


def rotate(values, places):
    inverse = 1.0 / ROPE_BASE ** (jnp.arange(0, HD, 2).astype(jnp.float32) / HD)
    angles = places.astype(jnp.float32)[:, None] * inverse[None, :]
    cosine = jnp.concatenate([jnp.cos(angles), jnp.cos(angles)], axis=-1)[:, None, :]
    sine = jnp.concatenate([jnp.sin(angles), jnp.sin(angles)], axis=-1)[:, None, :]
    first_half = values[..., : HD // 2]
    second_half = values[..., HD // 2 :]
    turned = jnp.concatenate([-second_half, first_half], axis=-1)
    return values * cosine + turned * sine


def absorb(state, queries, block_keys, block_values, allowed, scale):
    running_max, running_sum, output = state
    scores = (
        jnp.einsum("qcgd,kcd->cgqk", queries, block_keys, preferred_element_type=jnp.float32)
        * scale
    )
    scores = jnp.where(allowed[None, None], scores, FLOOR_SCORE)
    new_max = jnp.maximum(running_max, jnp.max(scores, axis=-1))
    factor = jnp.exp(running_max - new_max)
    weights = jnp.where(allowed[None, None], jnp.exp(scores - new_max[..., None]), 0.0)
    running_sum = running_sum * factor + jnp.sum(weights, axis=-1)
    mixed = jnp.einsum(
        "cgqk,kcd->qcgd",
        weights.astype(jnp.bfloat16),
        block_values,
        preferred_element_type=jnp.float32,
    )
    output = output * jnp.transpose(factor, (2, 0, 1))[..., None] + mixed
    return (new_max, running_sum, output)


def output_rows(w_out):
    parts = lax.axis_size("tp")
    depth = lax.axis_size("z")
    rows, width = w_out.shape
    share = rows // parts
    chunks = jnp.broadcast_to(w_out.reshape(1, parts, share, width), (depth, parts, share, width))
    pieces = lax.all_to_all(
        chunks.reshape(depth * parts, share, width), ("z", "tp"), 0, 0, tiled=True
    )
    near = jnp.transpose(pieces.reshape(depth, parts, share, width), (0, 2, 1, 3))
    near = near.reshape(depth * share, parts, width)
    return lax.all_gather(near, ("x", "core"), axis=0, tiled=True), share


def shards(q_new, k_new, v_new, k_cache, v_cache, lengths, page_table, w_out):
    own_rows = q_new.shape[0]
    all_rows = 2 * own_rows
    local_heads = k_new.shape[1] // HD
    pages_local = k_cache.shape[0]
    page_rows = k_cache.shape[1]
    scale = 1.0 / math.sqrt(HD)
    weights_mine, share = output_rows(w_out)
    device_row = (lax.axis_index("z") * lax.axis_size("x") + lax.axis_index("x")) * lax.axis_size(
        "core"
    ) + lax.axis_index("core")
    parity = device_row % 2
    request = device_row // 2
    length = lengths[request]
    own_places = length + parity * own_rows + jnp.arange(own_rows)
    own_queries = rotate(
        q_new.reshape(own_rows, local_heads * GROUP, HD).astype(jnp.float32), own_places
    ).astype(jnp.bfloat16)
    own_keys = rotate(
        k_new.reshape(own_rows, local_heads, HD).astype(jnp.float32), own_places
    ).astype(jnp.bfloat16)
    own_values = v_new.reshape(own_rows, local_heads, HD)
    query_heads = own_queries.shape[1]
    peer_pack = from_partner(
        jnp.concatenate([own_queries, own_keys, own_values], axis=1), "core", 0
    )
    peer_queries = peer_pack[:, :query_heads]
    peer_keys = peer_pack[:, query_heads : query_heads + local_heads]
    peer_values = peer_pack[:, query_heads + local_heads :]

    def ordered(mine, theirs):
        return jnp.where(
            parity == 0,
            jnp.concatenate([mine, theirs], axis=0),
            jnp.concatenate([theirs, mine], axis=0),
        )

    queries = ordered(own_queries, peer_queries).reshape(all_rows, local_heads, GROUP, HD)
    fresh_keys = ordered(own_keys, peer_keys)
    fresh_values = ordered(own_values, peer_values)
    token_index = jnp.arange(all_rows)
    causal = (token_index[None, :] <= token_index[:, None]) & (parity == 1)
    page_count = (length + page_rows - 1) // page_rows
    even_pages = (page_count + 1) // 2
    first_page = jnp.where(parity == 0, 0, even_pages)
    last_page = jnp.where(parity == 0, even_pages, page_count)
    table_row = page_table[request]
    logical = jnp.arange(table_row.shape[0])
    in_range = (logical >= first_page) & (logical < last_page)
    offset = device_row * pages_local
    slot_ids = jnp.arange(pages_local)
    match = in_range[:, None] & (table_row[:, None] - offset == slot_ids[None, :])
    used = jnp.any(match, axis=0)
    base = jnp.sum(jnp.where(match, logical[:, None], 0), axis=0) * page_rows
    key_places = (base[:, None] + jnp.arange(page_rows)[None, :]).reshape(-1)
    usable = jnp.repeat(used, page_rows) & (key_places < length)
    allowed = jnp.broadcast_to(usable[None, :], (all_rows, pages_local * page_rows))
    pool_keys = k_cache.reshape(pages_local * page_rows, local_heads, HD)
    pool_values = v_cache.reshape(pages_local * page_rows, local_heads, HD)
    half = pool_keys.shape[0] // 2

    def attend(start):
        state = (
            jnp.full((local_heads, GROUP, own_rows), FLOOR_SCORE, jnp.float32),
            jnp.zeros((local_heads, GROUP, own_rows), jnp.float32),
            jnp.zeros((own_rows, local_heads, GROUP, HD), jnp.float32),
        )
        rows_queries = lax.dynamic_slice_in_dim(queries, start, own_rows, 0)
        rows_causal = lax.dynamic_slice_in_dim(causal, start, own_rows, 0)
        state = absorb(state, rows_queries, fresh_keys, fresh_values, rows_causal, scale)
        for first in (0, half):
            state = absorb(
                state,
                rows_queries,
                pool_keys[first : first + half],
                pool_values[first : first + half],
                allowed[:own_rows, first : first + half],
                scale,
            )
        return state

    peer_start = (1 - parity) * own_rows
    own_start = parity * own_rows
    peer_max, peer_sum, peer_output = attend(peer_start)
    outgoing = (peer_output, peer_max, peer_sum)
    outgoing = jnp.concatenate(
        [
            outgoing[0].astype(jnp.bfloat16),
            jnp.transpose(outgoing[1], (2, 0, 1))[..., None].astype(jnp.bfloat16),
            jnp.transpose(outgoing[2], (2, 0, 1))[..., None].astype(jnp.bfloat16),
        ],
        axis=-1,
    )
    incoming = from_partner(outgoing, "core", 0).astype(jnp.float32)
    other_output = incoming[..., :HD]
    other_max = jnp.transpose(incoming[..., HD], (1, 2, 0))
    other_sum = jnp.transpose(incoming[..., HD + 1], (1, 2, 0))
    mine_max, mine_sum, mine_output = attend(own_start)
    joint_max = jnp.maximum(mine_max, other_max)
    mine_factor = jnp.exp(mine_max - joint_max)
    other_factor = jnp.exp(other_max - joint_max)
    joint_sum = mine_sum * mine_factor + other_sum * other_factor
    joint_output = (
        mine_output * jnp.transpose(mine_factor, (2, 0, 1))[..., None]
        + other_output * jnp.transpose(other_factor, (2, 0, 1))[..., None]
    )
    attention = (
        (joint_output / jnp.transpose(joint_sum, (2, 0, 1))[..., None])
        .reshape(own_rows, local_heads * GROUP * HD)
        .astype(jnp.bfloat16)
    )
    full_rows = lax.all_gather(attention[:, None], "tp", axis=1, tiled=True)
    projected = lax.dot_general(
        full_rows,
        weights_mine,
        (((1, 2), (1, 2)), ((), ())),
        preferred_element_type=jnp.float32,
    )
    depth = lax.axis_size("z")
    projected = projected.reshape(own_rows, -1, depth, share)
    projected = jnp.transpose(projected, (0, 2, 1, 3)).reshape(own_rows, -1, share)
    projected = projected.astype(jnp.bfloat16)
    gathered = lax.all_gather(projected, "tp", axis=2, tiled=True)
    return gathered.reshape(own_rows, -1)


def solution(mesh):
    in_specs = (
        P(ROWS, "tp"),
        P(ROWS, "tp"),
        P(ROWS, "tp"),
        P(ROWS, None, "tp"),
        P(ROWS, None, "tp"),
        P(),
        P(),
        P(ROWS, "tp"),
    )
    out_specs = P(ROWS, None)
    rows, parts = mesh.devices.shape
    cores = 2
    depth = 4 if rows % (4 * cores) == 0 else 1
    split = Mesh(mesh.devices.reshape(depth, rows // (depth * cores), cores, parts), ROWS + ("tp",))
    return jax.shard_map(shards, mesh=split, in_specs=in_specs, out_specs=out_specs, check_vma=False)
```

```python
import math

import jax
import jax.numpy as jnp
from jax import lax
from jax.sharding import Mesh
from jax.sharding import PartitionSpec as P

HD = 128
GROUP = 5
ROWS = ("z", "x", "core")


ROPE_BASE = 1000000.0
FLOOR_SCORE = -1e30


def from_partner(value, axis, distance):
    return lax.ppermute(value, axis, [(i, i ^ 1 << distance) for i in range(lax.axis_size(axis))])


def rotate(values, places):
    inverse = 1.0 / ROPE_BASE ** (jnp.arange(0, HD, 2).astype(jnp.float32) / HD)
    angles = places.astype(jnp.float32)[:, None] * inverse[None, :]
    cosine = jnp.concatenate([jnp.cos(angles), jnp.cos(angles)], axis=-1)[:, None, :]
    sine = jnp.concatenate([jnp.sin(angles), jnp.sin(angles)], axis=-1)[:, None, :]
    first_half = values[..., : HD // 2]
    second_half = values[..., HD // 2 :]
    turned = jnp.concatenate([-second_half, first_half], axis=-1)
    return values * cosine + turned * sine


def absorb(state, queries, block_keys, block_values, allowed, scale):
    running_max, running_sum, output = state
    scores = (
        jnp.einsum("qcgd,kcd->cgqk", queries, block_keys, preferred_element_type=jnp.float32)
        * scale
    )
    scores = jnp.where(allowed[None, None], scores, FLOOR_SCORE)
    new_max = jnp.maximum(running_max, jnp.max(scores, axis=-1))
    factor = jnp.exp(running_max - new_max)
    weights = jnp.where(allowed[None, None], jnp.exp(scores - new_max[..., None]), 0.0)
    running_sum = running_sum * factor + jnp.sum(weights, axis=-1)
    mixed = jnp.einsum(
        "cgqk,kcd->qcgd",
        weights.astype(jnp.bfloat16),
        block_values,
        preferred_element_type=jnp.float32,
    )
    output = output * jnp.transpose(factor, (2, 0, 1))[..., None] + mixed
    return (new_max, running_sum, output)


def output_rows(w_out):
    parts = lax.axis_size("tp")
    depth = lax.axis_size("z")
    rows, width = w_out.shape
    share = rows // parts
    chunks = jnp.broadcast_to(w_out.reshape(1, parts, share, width), (depth, parts, share, width))
    pieces = lax.all_to_all(
        chunks.reshape(depth * parts, share, width), ("z", "tp"), 0, 0, tiled=True
    )
    near = jnp.transpose(pieces.reshape(depth, parts, share, width), (0, 2, 1, 3))
    near = near.reshape(depth * share, parts, width)
    return lax.all_gather(near, ("x", "core"), axis=0, tiled=True), share


def shards(q_new, k_new, v_new, k_cache, v_cache, lengths, page_table, w_out):
    own_rows = q_new.shape[0]
    all_rows = 2 * own_rows
    local_heads = k_new.shape[1] // HD
    pages_local = k_cache.shape[0]
    page_rows = k_cache.shape[1]
    scale = 1.0 / math.sqrt(HD)
    weights_mine, share = output_rows(w_out)
    device_row = (lax.axis_index("z") * lax.axis_size("x") + lax.axis_index("x")) * lax.axis_size(
        "core"
    ) + lax.axis_index("core")
    parity = device_row % 2
    request = device_row // 2
    length = lengths[request]
    own_places = length + parity * own_rows + jnp.arange(own_rows)
    own_queries = rotate(
        q_new.reshape(own_rows, local_heads * GROUP, HD).astype(jnp.float32), own_places
    ).astype(jnp.bfloat16)
    own_keys = rotate(
        k_new.reshape(own_rows, local_heads, HD).astype(jnp.float32), own_places
    ).astype(jnp.bfloat16)
    own_values = v_new.reshape(own_rows, local_heads, HD)
    query_heads = own_queries.shape[1]
    peer_pack = from_partner(
        jnp.concatenate([own_queries, own_keys, own_values], axis=1), "core", 0
    )
    peer_queries = peer_pack[:, :query_heads]
    peer_keys = peer_pack[:, query_heads : query_heads + local_heads]
    peer_values = peer_pack[:, query_heads + local_heads :]

    def ordered(mine, theirs):
        return jnp.where(
            parity == 0,
            jnp.concatenate([mine, theirs], axis=0),
            jnp.concatenate([theirs, mine], axis=0),
        )

    queries = ordered(own_queries, peer_queries).reshape(all_rows, local_heads, GROUP, HD)
    fresh_keys = ordered(own_keys, peer_keys)
    fresh_values = ordered(own_values, peer_values)
    state = (
        jnp.full((local_heads, GROUP, all_rows), FLOOR_SCORE, jnp.float32),
        jnp.zeros((local_heads, GROUP, all_rows), jnp.float32),
        jnp.zeros((all_rows, local_heads, GROUP, HD), jnp.float32),
    )
    token_index = jnp.arange(all_rows)
    causal = (token_index[None, :] <= token_index[:, None]) & (parity == 1)
    page_count = (length + page_rows - 1) // page_rows
    even_pages = (page_count + 1) // 2
    first_page = jnp.where(parity == 0, 0, even_pages)
    last_page = jnp.where(parity == 0, even_pages, page_count)
    table_row = page_table[request]
    logical = jnp.arange(table_row.shape[0])
    in_range = (logical >= first_page) & (logical < last_page)
    offset = device_row * pages_local
    slot_ids = jnp.arange(pages_local)
    match = in_range[:, None] & (table_row[:, None] - offset == slot_ids[None, :])
    used = jnp.any(match, axis=0)
    base = jnp.sum(jnp.where(match, logical[:, None], 0), axis=0) * page_rows
    key_places = (base[:, None] + jnp.arange(page_rows)[None, :]).reshape(-1)
    usable = jnp.repeat(used, page_rows) & (key_places < length)
    allowed = jnp.broadcast_to(usable[None, :], (all_rows, pages_local * page_rows))
    pool_keys = k_cache.reshape(pages_local * page_rows, local_heads, HD)
    pool_values = v_cache.reshape(pages_local * page_rows, local_heads, HD)
    half = pool_keys.shape[0] // 2
    state = absorb(
        state,
        queries,
        jnp.concatenate([fresh_keys, pool_keys[:half]], axis=0),
        jnp.concatenate([fresh_values, pool_values[:half]], axis=0),
        jnp.concatenate([causal, allowed[:, :half]], axis=1),
        scale,
    )
    state = absorb(state, queries, pool_keys[half:], pool_values[half:], allowed[:, half:], scale)
    running_max, running_sum, output = state
    peer_start = (1 - parity) * own_rows
    own_start = parity * own_rows
    outgoing = (
        lax.dynamic_slice_in_dim(output, peer_start, own_rows, 0),
        lax.dynamic_slice_in_dim(running_max, peer_start, own_rows, 2),
        lax.dynamic_slice_in_dim(running_sum, peer_start, own_rows, 2),
    )
    outgoing = jnp.concatenate(
        [
            outgoing[0].astype(jnp.bfloat16),
            jnp.transpose(outgoing[1], (2, 0, 1))[..., None].astype(jnp.bfloat16),
            jnp.transpose(outgoing[2], (2, 0, 1))[..., None].astype(jnp.bfloat16),
        ],
        axis=-1,
    )
    incoming = from_partner(outgoing, "core", 0).astype(jnp.float32)
    other_output = incoming[..., :HD]
    other_max = jnp.transpose(incoming[..., HD], (1, 2, 0))
    other_sum = jnp.transpose(incoming[..., HD + 1], (1, 2, 0))
    mine_output = lax.dynamic_slice_in_dim(output, own_start, own_rows, 0)
    mine_max = lax.dynamic_slice_in_dim(running_max, own_start, own_rows, 2)
    mine_sum = lax.dynamic_slice_in_dim(running_sum, own_start, own_rows, 2)
    joint_max = jnp.maximum(mine_max, other_max)
    mine_factor = jnp.exp(mine_max - joint_max)
    other_factor = jnp.exp(other_max - joint_max)
    joint_sum = mine_sum * mine_factor + other_sum * other_factor
    joint_output = (
        mine_output * jnp.transpose(mine_factor, (2, 0, 1))[..., None]
        + other_output * jnp.transpose(other_factor, (2, 0, 1))[..., None]
    )
    attention = (
        (joint_output / jnp.transpose(joint_sum, (2, 0, 1))[..., None])
        .reshape(own_rows, local_heads * GROUP * HD)
        .astype(jnp.bfloat16)
    )
    full_rows = lax.all_gather(attention[:, None], "tp", axis=1, tiled=True)
    projected = lax.dot_general(
        full_rows,
        weights_mine,
        (((1, 2), (1, 2)), ((), ())),
        preferred_element_type=jnp.float32,
    )
    depth = lax.axis_size("z")
    projected = projected.reshape(own_rows, -1, depth, share)
    projected = jnp.transpose(projected, (0, 2, 1, 3)).reshape(own_rows, -1, share)
    projected = projected.astype(jnp.bfloat16)
    gathered = lax.all_gather(projected, "tp", axis=2, tiled=True)
    return gathered.reshape(own_rows, -1)


def solution(mesh):
    in_specs = (
        P(ROWS, "tp"),
        P(ROWS, "tp"),
        P(ROWS, "tp"),
        P(ROWS, None, "tp"),
        P(ROWS, None, "tp"),
        P(),
        P(),
        P(ROWS, "tp"),
    )
    out_specs = P(ROWS, None)
    rows, parts = mesh.devices.shape
    cores = 2
    depth = 4 if rows % (4 * cores) == 0 else 1
    split = Mesh(mesh.devices.reshape(depth, rows // (depth * cores), cores, parts), ROWS + ("tp",))
    return jax.shard_map(shards, mesh=split, in_specs=in_specs, out_specs=out_specs, check_vma=False)
```

```python
import math

import jax
import jax.numpy as jnp
from jax import lax
from jax.sharding import Mesh
from jax.sharding import PartitionSpec as P

HD = 128
GROUP = 5
ROWS = ("z", "x", "core")


ROPE_BASE = 1000000.0
FLOOR_SCORE = -1e30


def from_partner(value, axis, distance):
    return lax.ppermute(value, axis, [(i, i ^ 1 << distance) for i in range(lax.axis_size(axis))])


def rotate(values, places):
    inverse = 1.0 / ROPE_BASE ** (jnp.arange(0, HD, 2).astype(jnp.float32) / HD)
    angles = places.astype(jnp.float32)[:, None] * inverse[None, :]
    cosine = jnp.concatenate([jnp.cos(angles), jnp.cos(angles)], axis=-1)[:, None, :]
    sine = jnp.concatenate([jnp.sin(angles), jnp.sin(angles)], axis=-1)[:, None, :]
    first_half = values[..., : HD // 2]
    second_half = values[..., HD // 2 :]
    turned = jnp.concatenate([-second_half, first_half], axis=-1)
    return values * cosine + turned * sine


def absorb(state, queries, block_keys, block_values, allowed, scale):
    running_max, running_sum, output = state
    scores = (
        jnp.einsum("qcgd,kcd->cgqk", queries, block_keys, preferred_element_type=jnp.float32)
        * scale
    )
    scores = jnp.where(allowed[None, None], scores, FLOOR_SCORE)
    new_max = jnp.maximum(running_max, jnp.max(scores, axis=-1))
    factor = jnp.exp(running_max - new_max)
    weights = jnp.where(allowed[None, None], jnp.exp(scores - new_max[..., None]), 0.0)
    running_sum = running_sum * factor + jnp.sum(weights, axis=-1)
    mixed = jnp.einsum(
        "cgqk,kcd->qcgd",
        weights.astype(jnp.bfloat16),
        block_values,
        preferred_element_type=jnp.float32,
    )
    output = output * jnp.transpose(factor, (2, 0, 1))[..., None] + mixed
    return (new_max, running_sum, output)


def output_rows(w_out):
    parts = lax.axis_size("tp")
    rows, width = w_out.shape
    share = rows // parts
    pieces = lax.all_to_all(w_out.reshape(parts, share, width), "tp", 0, 0, tiled=True)
    mine = jnp.transpose(pieces, (1, 0, 2))
    near = lax.all_gather(mine, "z", axis=0, tiled=True)
    return lax.all_gather(near, ("x", "core"), axis=0, tiled=True), share


def shards(q_new, k_new, v_new, k_cache, v_cache, lengths, page_table, w_out):
    own_rows = q_new.shape[0]
    all_rows = 2 * own_rows
    local_heads = k_new.shape[1] // HD
    pages_local = k_cache.shape[0]
    page_rows = k_cache.shape[1]
    scale = 1.0 / math.sqrt(HD)
    weights_mine, share = output_rows(w_out)
    device_row = (lax.axis_index("z") * lax.axis_size("x") + lax.axis_index("x")) * lax.axis_size(
        "core"
    ) + lax.axis_index("core")
    parity = device_row % 2
    request = device_row // 2
    length = lengths[request]
    own_places = length + parity * own_rows + jnp.arange(own_rows)
    own_queries = rotate(
        q_new.reshape(own_rows, local_heads * GROUP, HD).astype(jnp.float32), own_places
    ).astype(jnp.bfloat16)
    own_keys = rotate(
        k_new.reshape(own_rows, local_heads, HD).astype(jnp.float32), own_places
    ).astype(jnp.bfloat16)
    own_values = v_new.reshape(own_rows, local_heads, HD)
    query_heads = own_queries.shape[1]
    peer_pack = from_partner(
        jnp.concatenate([own_queries, own_keys, own_values], axis=1), "core", 0
    )
    peer_queries = peer_pack[:, :query_heads]
    peer_keys = peer_pack[:, query_heads : query_heads + local_heads]
    peer_values = peer_pack[:, query_heads + local_heads :]

    def ordered(mine, theirs):
        return jnp.where(
            parity == 0,
            jnp.concatenate([mine, theirs], axis=0),
            jnp.concatenate([theirs, mine], axis=0),
        )

    queries = ordered(own_queries, peer_queries).reshape(all_rows, local_heads, GROUP, HD)
    fresh_keys = ordered(own_keys, peer_keys)
    fresh_values = ordered(own_values, peer_values)
    state = (
        jnp.full((local_heads, GROUP, all_rows), FLOOR_SCORE, jnp.float32),
        jnp.zeros((local_heads, GROUP, all_rows), jnp.float32),
        jnp.zeros((all_rows, local_heads, GROUP, HD), jnp.float32),
    )
    token_index = jnp.arange(all_rows)
    causal = (token_index[None, :] <= token_index[:, None]) & (parity == 1)
    state = absorb(state, queries, fresh_keys, fresh_values, causal, scale)
    page_count = (length + page_rows - 1) // page_rows
    even_pages = (page_count + 1) // 2
    first_page = jnp.where(parity == 0, 0, even_pages)
    last_page = jnp.where(parity == 0, even_pages, page_count)
    table_row = page_table[request]
    logical = jnp.arange(table_row.shape[0])
    in_range = (logical >= first_page) & (logical < last_page)
    offset = device_row * pages_local
    slot_ids = jnp.arange(pages_local)
    match = in_range[:, None] & (table_row[:, None] - offset == slot_ids[None, :])
    used = jnp.any(match, axis=0)
    base = jnp.sum(jnp.where(match, logical[:, None], 0), axis=0) * page_rows
    key_places = (base[:, None] + jnp.arange(page_rows)[None, :]).reshape(-1)
    usable = jnp.repeat(used, page_rows) & (key_places < length)
    allowed = jnp.broadcast_to(usable[None, :], (all_rows, pages_local * page_rows))
    pool_keys = k_cache.reshape(pages_local * page_rows, local_heads, HD)
    pool_values = v_cache.reshape(pages_local * page_rows, local_heads, HD)
    half = pool_keys.shape[0] // 2
    for start in (0, half):
        state = absorb(
            state,
            queries,
            pool_keys[start : start + half],
            pool_values[start : start + half],
            allowed[:, start : start + half],
            scale,
        )
    running_max, running_sum, output = state
    peer_start = (1 - parity) * own_rows
    own_start = parity * own_rows
    outgoing = (
        lax.dynamic_slice_in_dim(output, peer_start, own_rows, 0),
        lax.dynamic_slice_in_dim(running_max, peer_start, own_rows, 2),
        lax.dynamic_slice_in_dim(running_sum, peer_start, own_rows, 2),
    )
    outgoing = jnp.concatenate(
        [
            outgoing[0].astype(jnp.bfloat16),
            jnp.transpose(outgoing[1], (2, 0, 1))[..., None].astype(jnp.bfloat16),
            jnp.transpose(outgoing[2], (2, 0, 1))[..., None].astype(jnp.bfloat16),
        ],
        axis=-1,
    )
    incoming = from_partner(outgoing, "core", 0).astype(jnp.float32)
    other_output = incoming[..., :HD]
    other_max = jnp.transpose(incoming[..., HD], (1, 2, 0))
    other_sum = jnp.transpose(incoming[..., HD + 1], (1, 2, 0))
    mine_output = lax.dynamic_slice_in_dim(output, own_start, own_rows, 0)
    mine_max = lax.dynamic_slice_in_dim(running_max, own_start, own_rows, 2)
    mine_sum = lax.dynamic_slice_in_dim(running_sum, own_start, own_rows, 2)
    joint_max = jnp.maximum(mine_max, other_max)
    mine_factor = jnp.exp(mine_max - joint_max)
    other_factor = jnp.exp(other_max - joint_max)
    joint_sum = mine_sum * mine_factor + other_sum * other_factor
    joint_output = (
        mine_output * jnp.transpose(mine_factor, (2, 0, 1))[..., None]
        + other_output * jnp.transpose(other_factor, (2, 0, 1))[..., None]
    )
    attention = (
        (joint_output / jnp.transpose(joint_sum, (2, 0, 1))[..., None])
        .reshape(own_rows, local_heads * GROUP * HD)
        .astype(jnp.bfloat16)
    )
    full_rows = lax.all_gather(attention[:, None], "tp", axis=1, tiled=True)
    projected = lax.dot_general(
        full_rows,
        weights_mine,
        (((1, 2), (1, 2)), ((), ())),
        preferred_element_type=jnp.float32,
    )
    depth = lax.axis_size("z")
    projected = projected.reshape(own_rows, -1, depth, share)
    projected = jnp.transpose(projected, (0, 2, 1, 3)).reshape(own_rows, -1, share)
    projected = projected.astype(jnp.bfloat16)
    gathered = lax.all_gather(projected, "tp", axis=2, tiled=True)
    return gathered.reshape(own_rows, -1)


def solution(mesh):
    in_specs = (
        P(ROWS, "tp"),
        P(ROWS, "tp"),
        P(ROWS, "tp"),
        P(ROWS, None, "tp"),
        P(ROWS, None, "tp"),
        P(),
        P(),
        P(ROWS, "tp"),
    )
    out_specs = P(ROWS, None)
    rows, parts = mesh.devices.shape
    cores = 2
    depth = 4 if rows % (4 * cores) == 0 else 1
    split = Mesh(mesh.devices.reshape(depth, rows // (depth * cores), cores, parts), ROWS + ("tp",))
    return jax.shard_map(shards, mesh=split, in_specs=in_specs, out_specs=out_specs, check_vma=False)
```
